32 devices in a mesh: pb: 8 (over z, x), ka: 4 (over y, core).
Axes of the slice: x: 2, y: 2, z: 4, core: 2. Of those that a mesh axis runs over, the one named last changes fastest.
Arguments:
- queries: bfloat16 [8192, 512], P('pb'), may hold values from -80 to 80
- key_cache: bfloat16 [8192, 128], P(('ka', 'pb')), may hold values from -4.1 to 4.1
- value_cache: bfloat16 [8192, 128], P(('ka', 'pb')), may hold values from -4 to 4
- block_list: int32 [64, 32], P('pb'), may hold values from 0 to 63, as said below
- block_count: int32 [64], P('pb'), may hold values from 1 to 32, as said below
Outputs:
- attended: bfloat16 [8192, 512], P(('pb', 'ka'))
The draws below stay inside these ranges and needn't reach their ends.
Inputs may be any that keep to these rules, and one draw needn't show every extreme that they name: `block_list`: entries of row qb before block_count[qb] are distinct blocks at most qb, and qb itself is among them. They are the blocks v at most qb of one set of 16 vertical blocks, then the blocks qb - o at least 0 (and not already listed) of one set of 16 slash offsets; both sets contain 0 and lie below 16. Later entries equal qb. `block_count`: the number of distinct listed blocks of each query block.
All inputs are finite; a program needn't handle non-finite values.
Results may differ from the reference program's by a relative error of at most 0.0046.
Values may be sent and summed in bfloat16 or wider, within the bound.
No kernel may reach another device: no remote copies, remote signals or barrier semaphores. Data moves between devices by JAX's collectives and lax.ppermute only.
A program may use at most 128 MiB of HBM per device.

```python
import math
import jax
import jax.numpy as jnp
from jax import lax

HD = 128
QH = 4
BLK = 128
LIST = 32
NV = 16
NQB = 64
SEQ = 8192
N_KA = 4


def build_lists(key):
    vertical_key, offset_key = jax.random.split(jax.random.fold_in(key, 11))
    quarter = NQB // 4
    verticals = jnp.concatenate([jnp.zeros((1,), jnp.int32), 1 + jax.random.permutation(vertical_key, quarter - 1)[:NV - 1].astype(jnp.int32)])
    offsets = jnp.concatenate([jnp.zeros((1,), jnp.int32), 1 + jax.random.permutation(offset_key, quarter - 1)[:LIST - NV - 1].astype(jnp.int32)])
    block_ids = jnp.arange(NQB, dtype=jnp.int32)[:, None]
    vertical_ok = verticals[None, :] <= block_ids
    slash_blocks = block_ids - offsets[None, :]
    repeated = jnp.any((slash_blocks[:, :, None] == verticals[None, None, :]) & vertical_ok[:, None, :], axis=2)
    slash_ok = (slash_blocks >= 0) & jnp.logical_not(repeated)
    candidate = jnp.concatenate([jnp.broadcast_to(verticals[None, :], (NQB, NV)), slash_blocks], axis=1)
    usable = jnp.concatenate([vertical_ok, slash_ok], axis=1)
    slot_ids = jnp.arange(LIST, dtype=jnp.int32)[None, :]
    ordering = jnp.argsort(jnp.where(usable, slot_ids, LIST + slot_ids), axis=1)
    arranged = jnp.take_along_axis(candidate, ordering, axis=1)
    live_count = jnp.sum(usable.astype(jnp.int32), axis=1)
    listed = jnp.where(slot_ids < live_count[:, None], arranged, block_ids)
    return (listed.astype(jnp.int32), live_count.astype(jnp.int32))


def draw_block_list(key, part):
    return build_lists(key)[0]


def draw_block_count(key, part):
    return build_lists(key)[1]


def draw_base(key):
    return jnp.clip(jax.random.normal(jax.random.fold_in(key, 21), (SEQ, HD), jnp.float32), -4.0, 4.0)


def draw_key_cache(key, part):
    base_keys = draw_base(key)
    return base_keys.astype(jnp.bfloat16)


def draw_queries(key, part):
    values = jnp.clip(jax.random.normal(jax.random.fold_in(key, 22), (SEQ, QH * HD), jnp.float32), -4.0, 4.0)
    return values.astype(jnp.bfloat16)


def steps_of(rng, shape, shards, low, largest):
    level, own = 1.0, jax.random.fold_in(rng, 6)
    for dim, parts in shards:
        draws = jnp.exp(jax.random.uniform(jax.random.fold_in(own, dim), (parts,), jnp.float32, low / len(shards), largest / len(shards)))
        level = level * jnp.repeat(draws, shape[dim] // parts).reshape([-1 if axis == dim else 1 for axis in range(len(shape))])
    return level


def normal_values(rng, dims, spread, most, shards=(), kind=jnp.bfloat16):
    values = jax.random.normal(rng, dims, jnp.float32) * spread
    if len(shards) > 0:
        values = steps_of(rng, dims, shards, -0.22, 0.18) * values
    return jnp.clip(values, min=-most, max=most).astype(kind)


def setup_inputs(seed: int = 0) -> dict:
    keys = jax.random.split(jax.random.key(seed), 6)
    queries = draw_queries(jax.random.fold_in(keys[5], 71), 0)
    key_cache = draw_key_cache(jax.random.fold_in(keys[5], 71), 0)
    value_cache = normal_values(keys[2], (SEQ, HD), 1.0, 4.0, ((0, 32),))
    block_list = draw_block_list(jax.random.fold_in(keys[5], 71), 0)
    block_count = draw_block_count(jax.random.fold_in(keys[5], 71), 0)
    return {"queries": queries, "key_cache": key_cache, "value_cache": value_cache, "block_list": block_list, "block_count": block_count}


masked_score = -1e+30

def reference(queries, key_cache, value_cache, block_list, block_count):
    score_scale = 1.0 / math.sqrt(HD)
    total_blocks = block_list.shape[0]
    shard_width = total_blocks // N_KA
    key_blocks = key_cache.reshape(total_blocks, BLK, HD)
    value_blocks = value_cache.reshape(total_blocks, BLK, HD)
    slot_ids = jnp.arange(LIST, dtype=jnp.int32)
    shard_ids = jnp.arange(N_KA, dtype=jnp.int32)
    position = jnp.arange(BLK, dtype=jnp.int32)

    def one_block(block_pos):
        query_rows = lax.dynamic_slice_in_dim(queries, block_pos * BLK, BLK, 0)
        query_rows = query_rows.reshape(BLK, QH, HD).astype(jnp.float32)
        listed = block_list[block_pos]
        live_count = block_count[block_pos]
        key_tiles = key_blocks[listed].astype(jnp.float32)
        value_tiles = value_blocks[listed].astype(jnp.float32)
        scores = jnp.einsum('qhd,skd->hqsk', query_rows, key_tiles) * score_scale
        earlier = (listed < block_pos)[None, :, None]
        diagonal = (listed == block_pos)[None, :, None] & (position[None, None, :] <= position[:, None, None])
        valid = (slot_ids < live_count)[None, :, None] & (earlier | diagonal)
        masked = jnp.where(valid[None], scores, masked_score)
        slot_peak = lax.optimization_barrier(jnp.max(masked, axis=3))
        shard_of = (listed // shard_width).astype(jnp.int32)
        in_shard = shard_of[:, None] == shard_ids[None, :]
        shard_peak = lax.optimization_barrier(jnp.max(jnp.where(in_shard[None, None], slot_peak[..., None], masked_score), axis=2))
        peak_slot = jnp.take(shard_peak, shard_of, axis=2)
        weights = jnp.where(valid[None], jnp.exp(scores - peak_slot[..., None]), 0.0)
        membership = in_shard.astype(jnp.float32)
        shard_sum = jnp.einsum('hqs,sj->hqj', lax.optimization_barrier(jnp.sum(weights, axis=3)), membership)
        rounded = lax.optimization_barrier(weights.astype(jnp.bfloat16)).astype(jnp.float32)
        per_slot = jnp.einsum('hqsk,skd->hqsd', rounded, value_tiles)
        shard_out = jnp.einsum('hqsd,sj->hqjd', per_slot, membership)
        overall = lax.optimization_barrier(jnp.max(shard_peak, axis=2))
        factor = jnp.exp(shard_peak - overall[..., None])
        numerator = jnp.einsum('hqjd,hqj->hqd', shard_out, factor)
        denominator = lax.optimization_barrier(jnp.sum(shard_sum * factor, axis=2))
        result = numerator / denominator[..., None]
        return jnp.transpose(result, (1, 0, 2)).reshape(BLK, QH * HD).astype(jnp.bfloat16)
    blocks_out = lax.map(one_block, jnp.arange(total_blocks, dtype=jnp.int32))
    return blocks_out.reshape(total_blocks * BLK, QH * HD)
```

```python
import functools
import math

import jax
import jax.numpy as jnp
from jax import lax
from jax.experimental import pallas as pl
from jax.experimental.pallas import tpu as pltpu
from jax.sharding import PartitionSpec as P

HD = 128
QH = 4
BLK = 128

masked_score = -1e30


def gather_pb(local, n_pb):
    p = lax.axis_index("pb")
    held = local[None]
    step = 1
    while step < n_pb:
        other = lax.ppermute(held, "pb", [(i, i ^ step) for i in range(n_pb)])
        upper = (p // step) % 2 == 1
        held = jnp.where(
            upper,
            jnp.concatenate([other, held], axis=0),
            jnp.concatenate([held, other], axis=0),
        )
        step *= 2
    return held.reshape(-1, local.shape[1])


def attend_kernel(bl_ref, cnt_ref, qb_ref, q_ref, kv_hbm, out_ref, kvbuf, sems, *, n_local, scale):
    qb0 = qb_ref[0]

    def copy(j, s):
        blk = bl_ref[j, s]
        start = pl.multiple_of(blk * BLK, BLK)
        return pltpu.make_async_copy(kv_hbm.at[pl.ds(start, BLK), :], kvbuf.at[j, s], sems.at[j, s])

    for j in range(n_local):
        def issue(s, c, j=j):
            copy(j, s).start()
            return c

        lax.fori_loop(0, cnt_ref[j], issue, 0)

    rows = QH * BLK
    rowpos = lax.broadcasted_iota(jnp.int32, (rows, BLK), 0) % BLK
    col = lax.broadcasted_iota(jnp.int32, (rows, BLK), 1)
    causal = col <= rowpos

    for j in range(n_local):
        qb = qb0 + j
        qrows = q_ref[j * BLK:(j + 1) * BLK, :]
        qs = jnp.concatenate([qrows[:, h * HD:(h + 1) * HD] for h in range(QH)], axis=0)

        def body(s, carry, j=j, qb=qb, qs=qs):
            m, l, acc = carry
            copy(j, s).wait()
            kvb = kvbuf[j, s]
            k = kvb[:, :HD]
            v = kvb[:, HD:]
            blk = bl_ref[j, s]
            sc = lax.dot_general(qs, k, (((1,), (1,)), ((), ())), preferred_element_type=jnp.float32) * scale
            valid = jnp.logical_or(blk < qb, jnp.logical_and(blk == qb, causal))
            masked = jnp.where(valid, sc, masked_score)
            m_new = jnp.maximum(m, jnp.max(masked, axis=1, keepdims=True))
            alpha = jnp.exp(m - m_new)
            w = jnp.where(valid, jnp.exp(sc - m_new), 0.0)
            l = alpha * l + jnp.sum(w, axis=1, keepdims=True)
            acc = alpha * acc + jnp.dot(w.astype(jnp.bfloat16), v, preferred_element_type=jnp.float32)
            return m_new, l, acc

        init = (
            jnp.full((rows, 1), masked_score, jnp.float32),
            jnp.zeros((rows, 1), jnp.float32),
            jnp.zeros((rows, HD), jnp.float32),
        )
        m, l, acc = lax.fori_loop(0, cnt_ref[j], body, init)
        res = (acc / l).astype(out_ref.dtype)
        for h in range(QH):
            out_ref[j * BLK:(j + 1) * BLK, h * HD:(h + 1) * HD] = res[h * BLK:(h + 1) * BLK, :]


def shards(queries, key_cache, value_cache, block_list, block_count, *, n_pb, n_ka):
    kv_local = jnp.concatenate([key_cache, value_cache], axis=1)
    shard = gather_pb(kv_local, n_pb)
    kv_all = lax.all_gather(shard, "ka", axis=0, tiled=True)

    p = lax.axis_index("pb")
    k = lax.axis_index("ka")
    rows_mine = queries.shape[0] // n_ka
    n_local = rows_mine // BLK
    listed = block_list.shape[1]
    q_mine = lax.dynamic_slice_in_dim(queries, k * rows_mine, rows_mine, 0)
    bl_mine = lax.dynamic_slice_in_dim(block_list, k * n_local, n_local, 0)
    cnt_mine = lax.dynamic_slice_in_dim(block_count, k * n_local, n_local, 0)
    qb0 = ((p * n_ka + k) * n_local).astype(jnp.int32).reshape(1)

    kernel = functools.partial(attend_kernel, n_local=n_local, scale=1.0 / math.sqrt(HD))
    return pl.pallas_call(
        kernel,
        out_shape=jax.ShapeDtypeStruct((rows_mine, queries.shape[1]), jnp.bfloat16),
        grid_spec=pltpu.PrefetchScalarGridSpec(
            num_scalar_prefetch=3,
            grid=(1,),
            in_specs=[
                pl.BlockSpec((rows_mine, queries.shape[1]), lambda i, *_: (0, 0)),
                pl.BlockSpec(memory_space=pl.ANY),
            ],
            out_specs=pl.BlockSpec((rows_mine, queries.shape[1]), lambda i, *_: (0, 0)),
            scratch_shapes=[
                pltpu.VMEM((n_local, listed, BLK, kv_local.shape[1]), jnp.bfloat16),
                pltpu.SemaphoreType.DMA((n_local, listed)),
            ],
        ),
        compiler_params=pltpu.CompilerParams(vmem_limit_bytes=48 * 1024 * 1024),
    )(bl_mine, cnt_mine, qb0, q_mine, kv_all)


def solution(mesh):
    placed = (P("pb", None), P(("ka", "pb"), None), P(("ka", "pb"), None), P("pb", None), P("pb"))
    body = functools.partial(shards, n_pb=mesh.shape["pb"], n_ka=mesh.shape["ka"])
    return jax.shard_map(
        body, mesh=mesh, in_specs=placed, out_specs=P(("pb", "ka"), None), check_vma=False
    )
```

```python
import functools
import math

import jax
import jax.numpy as jnp
from jax import lax
from jax.experimental import pallas as pl
from jax.experimental.pallas import tpu as pltpu
from jax.sharding import PartitionSpec as P

HD = 128
QH = 4
BLK = 128

masked_score = -1e30


def gather_axis(local, axis, n):
    idx = lax.axis_index(axis)
    bits = n.bit_length() - 1
    held = local.reshape((1,) * bits + local.shape)
    for t in range(bits):
        b = n >> (t + 1)
        other = lax.ppermute(held, axis, [(i, i ^ b) for i in range(n)])
        upper = (idx // b) % 2 == 1
        held = jnp.where(
            upper,
            jnp.concatenate([other, held], axis=t),
            jnp.concatenate([held, other], axis=t),
        )
    return held.reshape((n * local.shape[0],) + local.shape[1:])


def attend_kernel(bl_ref, cnt_ref, qb_ref, q_ref, kv_hbm, out_ref, kvbuf, sems, *, n_local, scale):
    qb0 = qb_ref[0]

    def copy(j, s):
        blk = bl_ref[j, s]
        start = pl.multiple_of(blk * BLK, BLK)
        return pltpu.make_async_copy(kv_hbm.at[pl.ds(start, BLK), :], kvbuf.at[j, s], sems.at[j, s])

    for j in range(n_local):
        def issue(s, c, j=j):
            copy(j, s).start()
            return c

        lax.fori_loop(0, cnt_ref[j], issue, 0)

    rows = QH * BLK
    rowpos = lax.broadcasted_iota(jnp.int32, (rows, BLK), 0) % BLK
    col = lax.broadcasted_iota(jnp.int32, (rows, BLK), 1)
    causal = col <= rowpos

    for j in range(n_local):
        qb = qb0 + j
        qrows = q_ref[j * BLK:(j + 1) * BLK, :]
        qs = jnp.concatenate([qrows[:, h * HD:(h + 1) * HD] for h in range(QH)], axis=0)

        def body(s, carry, j=j, qb=qb, qs=qs):
            m, l, acc = carry
            copy(j, s).wait()
            kvb = kvbuf[j, s]
            k = kvb[:, :HD]
            v = kvb[:, HD:]
            blk = bl_ref[j, s]
            sc = lax.dot_general(qs, k, (((1,), (1,)), ((), ())), preferred_element_type=jnp.float32) * scale
            valid = jnp.logical_or(blk < qb, jnp.logical_and(blk == qb, causal))
            masked = jnp.where(valid, sc, masked_score)
            m_new = jnp.maximum(m, jnp.max(masked, axis=1, keepdims=True))
            alpha = jnp.exp(m - m_new)
            w = jnp.where(valid, jnp.exp(sc - m_new), 0.0)
            l = alpha * l + jnp.sum(w, axis=1, keepdims=True)
            acc = alpha * acc + jnp.dot(w.astype(jnp.bfloat16), v, preferred_element_type=jnp.float32)
            return m_new, l, acc

        init = (
            jnp.full((rows, 1), masked_score, jnp.float32),
            jnp.zeros((rows, 1), jnp.float32),
            jnp.zeros((rows, HD), jnp.float32),
        )
        m, l, acc = lax.fori_loop(0, cnt_ref[j], body, init)
        res = (acc / l).astype(out_ref.dtype)
        for h in range(QH):
            out_ref[j * BLK:(j + 1) * BLK, h * HD:(h + 1) * HD] = res[h * BLK:(h + 1) * BLK, :]


def shards(queries, key_cache, value_cache, block_list, block_count, *, n_pb, n_ka):
    kv_local = jnp.concatenate([key_cache, value_cache], axis=1)
    shard = gather_axis(kv_local, "pb", n_pb)
    kv_all = gather_axis(shard, "ka", n_ka)

    p = lax.axis_index("pb")
    k = lax.axis_index("ka")
    rows_mine = queries.shape[0] // n_ka
    n_local = rows_mine // BLK
    listed = block_list.shape[1]
    q_mine = lax.dynamic_slice_in_dim(queries, k * rows_mine, rows_mine, 0)
    bl_mine = lax.dynamic_slice_in_dim(block_list, k * n_local, n_local, 0)
    cnt_mine = lax.dynamic_slice_in_dim(block_count, k * n_local, n_local, 0)
    qb0 = ((p * n_ka + k) * n_local).astype(jnp.int32).reshape(1)

    kernel = functools.partial(attend_kernel, n_local=n_local, scale=1.0 / math.sqrt(HD))
    return pl.pallas_call(
        kernel,
        out_shape=jax.ShapeDtypeStruct((rows_mine, queries.shape[1]), jnp.bfloat16),
        grid_spec=pltpu.PrefetchScalarGridSpec(
            num_scalar_prefetch=3,
            grid=(1,),
            in_specs=[
                pl.BlockSpec((rows_mine, queries.shape[1]), lambda i, *_: (0, 0)),
                pl.BlockSpec(memory_space=pl.ANY),
            ],
            out_specs=pl.BlockSpec((rows_mine, queries.shape[1]), lambda i, *_: (0, 0)),
            scratch_shapes=[
                pltpu.VMEM((n_local, listed, BLK, kv_local.shape[1]), jnp.bfloat16),
                pltpu.SemaphoreType.DMA((n_local, listed)),
            ],
        ),
        compiler_params=pltpu.CompilerParams(vmem_limit_bytes=48 * 1024 * 1024),
    )(bl_mine, cnt_mine, qb0, q_mine, kv_all)


def solution(mesh):
    placed = (P("pb", None), P(("ka", "pb"), None), P(("ka", "pb"), None), P("pb", None), P("pb"))
    body = functools.partial(shards, n_pb=mesh.shape["pb"], n_ka=mesh.shape["ka"])
    return jax.shard_map(
        body, mesh=mesh, in_specs=placed, out_specs=P(("pb", "ka"), None), check_vma=False
    )
```

```python
import functools
import math

import jax
import jax.numpy as jnp
from jax import lax
from jax.experimental import pallas as pl
from jax.experimental.pallas import tpu as pltpu
from jax.sharding import PartitionSpec as P

HD = 128
QH = 4
BLK = 128

masked_score = -1e30


def gather_axis(local, axis, n):
    idx = lax.axis_index(axis)
    bits = n.bit_length() - 1
    held = local.reshape((1,) * bits + local.shape)
    for t in range(bits):
        b = n >> (t + 1)
        other = lax.ppermute(held, axis, [(i, i ^ b) for i in range(n)])
        upper = (idx // b) % 2 == 1
        held = jnp.where(
            upper,
            jnp.concatenate([other, held], axis=t),
            jnp.concatenate([held, other], axis=t),
        )
    return held.reshape((n * local.shape[0],) + local.shape[1:])


def attend_kernel(bl_ref, cnt_ref, qb_ref, q_ref, kv_hbm, out_ref, off_ref, kvbuf, dbuf, sems, dsems, *, n_local, group, scale):
    qb0 = qb_ref[0]
    width = kvbuf.shape[-1]

    def block_copy(blk, dst, sem):
        start = pl.multiple_of(blk * BLK, BLK)
        return pltpu.make_async_copy(kv_hbm.at[pl.ds(start, BLK), :], dst, sem)

    def copy(j, s):
        return block_copy(off_ref[j, s], kvbuf.at[j, s], sems.at[j, s])

    n_off = []
    for j in range(n_local):
        qb = qb0 + j
        block_copy(qb, dbuf.at[j], dsems.at[j]).start()

        def compact(s, n, j=j, qb=qb):
            b = bl_ref[j, s]
            off_ref[j, n] = b
            return n + (b != qb).astype(jnp.int32)

        n_j = lax.fori_loop(0, cnt_ref[j], compact, 0)
        n_off.append(n_j)

        def issue(s, c, j=j):
            copy(j, s).start()
            return c

        lax.fori_loop(0, n_j, issue, 0)

    rows = QH * BLK
    rowpos = lax.broadcasted_iota(jnp.int32, (rows, BLK), 0) % BLK
    col = lax.broadcasted_iota(jnp.int32, (rows, BLK), 1)
    causal = col <= rowpos
    dims = (((1,), (1,)), ((), ()))

    def update(qs, kvb, carry):
        m, l, acc = carry
        k = kvb[:, :HD]
        v = kvb[:, HD:]
        sc = lax.dot_general(qs, k, dims, preferred_element_type=jnp.float32) * scale
        m_new = jnp.maximum(m, jnp.max(sc, axis=1, keepdims=True))
        alpha = jnp.exp(m - m_new)
        w = jnp.exp(sc - m_new)
        l = alpha * l + jnp.sum(w, axis=1, keepdims=True)
        acc = alpha * acc + jnp.dot(w.astype(jnp.bfloat16), v, preferred_element_type=jnp.float32)
        return m_new, l, acc

    for j in range(n_local):
        qb = qb0 + j
        qrows = q_ref[j * BLK:(j + 1) * BLK, :]
        qs = jnp.concatenate([qrows[:, h * HD:(h + 1) * HD] for h in range(QH)], axis=0)

        block_copy(qb, dbuf.at[j], dsems.at[j]).wait()
        kvd = dbuf[j]
        sc = lax.dot_general(qs, kvd[:, :HD], dims, preferred_element_type=jnp.float32) * scale
        m = jnp.max(jnp.where(causal, sc, masked_score), axis=1, keepdims=True)
        w = jnp.where(causal, jnp.exp(sc - m), 0.0)
        l = jnp.sum(w, axis=1, keepdims=True)
        acc = jnp.dot(w.astype(jnp.bfloat16), kvd[:, HD:], preferred_element_type=jnp.float32)

        def grouped(g, carry, j=j, qs=qs):
            first = g * group
            for i in range(group):
                copy(j, first + i).wait()
            kvb = kvbuf[j, pl.ds(first, group)].reshape(group * BLK, width)
            return update(qs, kvb, carry)

        def single(s, carry, j=j, qs=qs):
            copy(j, s).wait()
            return update(qs, kvbuf[j, s], carry)

        n_groups = n_off[j] // group
        carry = lax.fori_loop(0, n_groups, grouped, (m, l, acc))
        m, l, acc = lax.fori_loop(n_groups * group, n_off[j], single, carry)
        res = (acc / l).astype(out_ref.dtype)
        for h in range(QH):
            out_ref[j * BLK:(j + 1) * BLK, h * HD:(h + 1) * HD] = res[h * BLK:(h + 1) * BLK, :]


def shards(queries, key_cache, value_cache, block_list, block_count, *, n_pb, n_ka):
    kv_local = jnp.concatenate([key_cache, value_cache], axis=1)
    shard = gather_axis(kv_local, "pb", n_pb)
    kv_all = gather_axis(shard, "ka", n_ka)

    p = lax.axis_index("pb")
    k = lax.axis_index("ka")
    rows_mine = queries.shape[0] // n_ka
    n_local = rows_mine // BLK
    listed = block_list.shape[1]
    q_mine = lax.dynamic_slice_in_dim(queries, k * rows_mine, rows_mine, 0)
    bl_mine = lax.dynamic_slice_in_dim(block_list, k * n_local, n_local, 0)
    cnt_mine = lax.dynamic_slice_in_dim(block_count, k * n_local, n_local, 0)
    qb0 = ((p * n_ka + k) * n_local).astype(jnp.int32).reshape(1)

    kernel = functools.partial(attend_kernel, n_local=n_local, group=4, scale=1.0 / math.sqrt(HD))
    return pl.pallas_call(
        kernel,
        out_shape=jax.ShapeDtypeStruct((rows_mine, queries.shape[1]), jnp.bfloat16),
        grid_spec=pltpu.PrefetchScalarGridSpec(
            num_scalar_prefetch=3,
            grid=(1,),
            in_specs=[
                pl.BlockSpec((rows_mine, queries.shape[1]), lambda i, *_: (0, 0)),
                pl.BlockSpec(memory_space=pl.ANY),
            ],
            out_specs=pl.BlockSpec((rows_mine, queries.shape[1]), lambda i, *_: (0, 0)),
            scratch_shapes=[
                pltpu.SMEM((n_local, listed), jnp.int32),
                pltpu.VMEM((n_local, listed, BLK, kv_local.shape[1]), jnp.bfloat16),
                pltpu.VMEM((n_local, BLK, kv_local.shape[1]), jnp.bfloat16),
                pltpu.SemaphoreType.DMA((n_local, listed)),
                pltpu.SemaphoreType.DMA((n_local,)),
            ],
        ),
        compiler_params=pltpu.CompilerParams(vmem_limit_bytes=48 * 1024 * 1024),
    )(bl_mine, cnt_mine, qb0, q_mine, kv_all)


def solution(mesh):
    placed = (P("pb", None), P(("ka", "pb"), None), P(("ka", "pb"), None), P("pb", None), P("pb"))
    body = functools.partial(shards, n_pb=mesh.shape["pb"], n_ka=mesh.shape["ka"])
    return jax.shard_map(
        body, mesh=mesh, in_specs=placed, out_specs=P(("pb", "ka"), None), check_vma=False
    )
```

```python
import functools
import math

import jax
import jax.numpy as jnp
from jax import lax
from jax.experimental import pallas as pl
from jax.experimental.pallas import tpu as pltpu
from jax.sharding import PartitionSpec as P

HD = 128
QH = 4
BLK = 128

masked_score = -1e30


def gather_axis(local, axis, n):
    idx = lax.axis_index(axis)
    bits = n.bit_length() - 1
    held = local.reshape((1,) * bits + local.shape)
    for t in range(bits):
        b = n >> (t + 1)
        other = lax.ppermute(held, axis, [(i, i ^ b) for i in range(n)])
        upper = (idx // b) % 2 == 1
        held = jnp.where(
            upper,
            jnp.concatenate([other, held], axis=t),
            jnp.concatenate([held, other], axis=t),
        )
    return held.reshape((n * local.shape[0],) + local.shape[1:])


def pieces_axis(local, axis, n):
    idx_pieces = {0: local}
    b = n // 2
    while b >= 1:
        for x in sorted(idx_pieces):
            idx_pieces[x | b] = lax.ppermute(idx_pieces[x], axis, [(i, i ^ b) for i in range(n)])
        b //= 2
    return [idx_pieces[x] for x in range(n)]


def attend_kernel(bl_ref, cnt_ref, qb_ref, q_ref, *rest, n_local, n_pieces, group, scale):
    kv_pieces = rest[:n_pieces]
    out_ref, off_ref, kvbuf, dbuf, sems, dsems = rest[n_pieces:]
    qb0 = qb_ref[0]
    me = qb_ref[1]
    width = kvbuf.shape[-1]
    per_piece = kv_pieces[0].shape[0] // BLK

    class block_copy:
        def __init__(self, blk, dst, sem):
            self.blk, self.dst, self.sem = blk, dst, sem

        def start(self):
            which = jnp.bitwise_xor(self.blk // per_piece, me)
            start = pl.multiple_of((self.blk % per_piece) * BLK, BLK)
            for x in range(n_pieces):
                @pl.when(which == x)
                def _(x=x, start=start):
                    pltpu.make_async_copy(kv_pieces[x].at[pl.ds(start, BLK), :], self.dst, self.sem).start()

        def wait(self):
            pltpu.make_async_copy(kv_pieces[0].at[pl.ds(0, BLK), :], self.dst, self.sem).wait()

    def copy(j, s):
        return block_copy(off_ref[j, s], kvbuf.at[j, s], sems.at[j, s])

    n_off = []
    for j in range(n_local):
        qb = qb0 + j
        block_copy(qb, dbuf.at[j], dsems.at[j]).start()

        def compact(s, n, j=j, qb=qb):
            b = bl_ref[j, s]
            off_ref[j, n] = b
            return n + (b != qb).astype(jnp.int32)

        n_j = lax.fori_loop(0, cnt_ref[j], compact, 0)
        n_off.append(n_j)

        def issue(s, c, j=j):
            copy(j, s).start()
            return c

        lax.fori_loop(0, n_j, issue, 0)

    rows = QH * BLK
    rowpos = lax.broadcasted_iota(jnp.int32, (rows, BLK), 0) % BLK
    col = lax.broadcasted_iota(jnp.int32, (rows, BLK), 1)
    causal = col <= rowpos
    dims = (((1,), (1,)), ((), ()))

    def update(qs, kvb, carry):
        m, l, acc = carry
        k = kvb[:, :HD]
        v = kvb[:, HD:]
        sc = lax.dot_general(qs, k, dims, preferred_element_type=jnp.float32) * scale
        m_new = jnp.maximum(m, jnp.max(sc, axis=1, keepdims=True))
        alpha = jnp.exp(m - m_new)
        w = jnp.exp(sc - m_new)
        l = alpha * l + jnp.sum(w, axis=1, keepdims=True)
        acc = alpha * acc + jnp.dot(w.astype(jnp.bfloat16), v, preferred_element_type=jnp.float32)
        return m_new, l, acc

    for j in range(n_local):
        qb = qb0 + j
        qrows = q_ref[j * BLK:(j + 1) * BLK, :]
        qs = jnp.concatenate([qrows[:, h * HD:(h + 1) * HD] for h in range(QH)], axis=0)

        block_copy(qb, dbuf.at[j], dsems.at[j]).wait()
        kvd = dbuf[j]
        sc = lax.dot_general(qs, kvd[:, :HD], dims, preferred_element_type=jnp.float32) * scale
        m = jnp.max(jnp.where(causal, sc, masked_score), axis=1, keepdims=True)
        w = jnp.where(causal, jnp.exp(sc - m), 0.0)
        l = jnp.sum(w, axis=1, keepdims=True)
        acc = jnp.dot(w.astype(jnp.bfloat16), kvd[:, HD:], preferred_element_type=jnp.float32)

        def grouped(g, carry, j=j, qs=qs):
            first = g * group
            for i in range(group):
                copy(j, first + i).wait()
            kvb = kvbuf[j, pl.ds(first, group)].reshape(group * BLK, width)
            return update(qs, kvb, carry)

        def single(s, carry, j=j, qs=qs):
            copy(j, s).wait()
            return update(qs, kvbuf[j, s], carry)

        n_groups = n_off[j] // group
        carry = lax.fori_loop(0, n_groups, grouped, (m, l, acc))
        m, l, acc = lax.fori_loop(n_groups * group, n_off[j], single, carry)
        res = (acc / l).astype(out_ref.dtype)
        for h in range(QH):
            out_ref[j * BLK:(j + 1) * BLK, h * HD:(h + 1) * HD] = res[h * BLK:(h + 1) * BLK, :]


def shards(queries, key_cache, value_cache, block_list, block_count, *, n_pb, n_ka):
    kv_local = jnp.concatenate([key_cache, value_cache], axis=1)
    shard = gather_axis(kv_local, "pb", n_pb)
    kv_pieces = pieces_axis(shard, "ka", n_ka)

    p = lax.axis_index("pb")
    k = lax.axis_index("ka")
    rows_mine = queries.shape[0] // n_ka
    n_local = rows_mine // BLK
    listed = block_list.shape[1]
    q_mine = lax.dynamic_slice_in_dim(queries, k * rows_mine, rows_mine, 0)
    bl_mine = lax.dynamic_slice_in_dim(block_list, k * n_local, n_local, 0)
    cnt_mine = lax.dynamic_slice_in_dim(block_count, k * n_local, n_local, 0)
    qb0 = jnp.stack([(p * n_ka + k) * n_local, k]).astype(jnp.int32)

    kernel = functools.partial(
        attend_kernel, n_local=n_local, n_pieces=n_ka, group=4, scale=1.0 / math.sqrt(HD)
    )
    return pl.pallas_call(
        kernel,
        out_shape=jax.ShapeDtypeStruct((rows_mine, queries.shape[1]), jnp.bfloat16),
        grid_spec=pltpu.PrefetchScalarGridSpec(
            num_scalar_prefetch=3,
            grid=(1,),
            in_specs=[
                pl.BlockSpec((rows_mine, queries.shape[1]), lambda i, *_: (0, 0)),
            ]
            + [pl.BlockSpec(memory_space=pl.ANY)] * n_ka,
            out_specs=pl.BlockSpec((rows_mine, queries.shape[1]), lambda i, *_: (0, 0)),
            scratch_shapes=[
                pltpu.SMEM((n_local, listed), jnp.int32),
                pltpu.VMEM((n_local, listed, BLK, kv_local.shape[1]), jnp.bfloat16),
                pltpu.VMEM((n_local, BLK, kv_local.shape[1]), jnp.bfloat16),
                pltpu.SemaphoreType.DMA((n_local, listed)),
                pltpu.SemaphoreType.DMA((n_local,)),
            ],
        ),
        compiler_params=pltpu.CompilerParams(vmem_limit_bytes=48 * 1024 * 1024),
    )(bl_mine, cnt_mine, qb0, q_mine, *kv_pieces)


def solution(mesh):
    placed = (P("pb", None), P(("ka", "pb"), None), P(("ka", "pb"), None), P("pb", None), P("pb"))
    body = functools.partial(shards, n_pb=mesh.shape["pb"], n_ka=mesh.shape["ka"])
    return jax.shard_map(
        body, mesh=mesh, in_specs=placed, out_specs=P(("pb", "ka"), None), check_vma=False
    )
```

```python
import functools
import math

import jax
import jax.numpy as jnp
from jax import lax
from jax.experimental import pallas as pl
from jax.experimental.pallas import tpu as pltpu
from jax.sharding import PartitionSpec as P

HD = 128
QH = 4
BLK = 128

masked_score = -1e30


def gather_axis(local, axis, n):
    idx = lax.axis_index(axis)
    bits = n.bit_length() - 1
    held = local.reshape((1,) * bits + local.shape)
    for t in range(bits):
        b = n >> (t + 1)
        other = lax.ppermute(held, axis, [(i, i ^ b) for i in range(n)])
        upper = (idx // b) % 2 == 1
        held = jnp.where(
            upper,
            jnp.concatenate([other, held], axis=t),
            jnp.concatenate([held, other], axis=t),
        )
    return held.reshape((n * local.shape[0],) + local.shape[1:])


def pieces_axis(local, axis, n):
    idx_pieces = {0: local}
    b = n // 2
    while b >= 1:
        for x in sorted(idx_pieces):
            idx_pieces[x | b] = lax.ppermute(idx_pieces[x], axis, [(i, i ^ b) for i in range(n)])
        b //= 2
    return [idx_pieces[x] for x in range(n)]


def attend_kernel(bl_ref, cnt_ref, qb_ref, q_ref, *rest, n_local, n_pieces, n_ka, group, scale):
    kv_pieces = rest[:n_pieces]
    out_ref, off_ref, kvbuf, dbuf, sems, dsems = rest[n_pieces:]
    qb0 = qb_ref[0]
    me = qb_ref[1]
    width = kvbuf.shape[-1]
    per_piece = kv_pieces[0].shape[0] // BLK
    n_half = n_pieces // n_ka

    class block_copy:
        def __init__(self, blk, dst, sem):
            self.blk, self.dst, self.sem = blk, dst, sem

        def start(self):
            per_shard = per_piece * n_half
            within = self.blk % per_shard
            which = (within % n_half) * n_ka + jnp.bitwise_xor(self.blk // per_shard, me)
            start = pl.multiple_of((within // n_half) * BLK, BLK)
            for x in range(n_pieces):
                @pl.when(which == x)
                def _(x=x, start=start):
                    pltpu.make_async_copy(kv_pieces[x].at[pl.ds(start, BLK), :], self.dst, self.sem).start()

        def wait(self):
            pltpu.make_async_copy(kv_pieces[0].at[pl.ds(0, BLK), :], self.dst, self.sem).wait()

    def copy(j, s):
        return block_copy(off_ref[j, s], kvbuf.at[j, s], sems.at[j, s])

    n_off = []
    for j in range(n_local):
        qb = qb0 + j
        block_copy(qb, dbuf.at[j], dsems.at[j]).start()

        def compact(s, n, j=j, qb=qb):
            b = bl_ref[j, s]
            off_ref[j, n] = b
            return n + (b != qb).astype(jnp.int32)

        n_j = lax.fori_loop(0, cnt_ref[j], compact, 0)
        n_off.append(n_j)

        def issue(s, c, j=j):
            copy(j, s).start()
            return c

        lax.fori_loop(0, n_j, issue, 0)

    rows = QH * BLK
    rowpos = lax.broadcasted_iota(jnp.int32, (rows, BLK), 0) % BLK
    col = lax.broadcasted_iota(jnp.int32, (rows, BLK), 1)
    causal = col <= rowpos
    dims = (((1,), (1,)), ((), ()))

    def update(qs, kvb, carry):
        m, l, acc = carry
        k = kvb[:, :HD]
        v = kvb[:, HD:]
        sc = lax.dot_general(qs, k, dims, preferred_element_type=jnp.float32) * scale
        m_new = jnp.maximum(m, jnp.max(sc, axis=1, keepdims=True))
        alpha = jnp.exp(m - m_new)
        w = jnp.exp(sc - m_new)
        l = alpha * l + jnp.sum(w, axis=1, keepdims=True)
        acc = alpha * acc + jnp.dot(w.astype(jnp.bfloat16), v, preferred_element_type=jnp.float32)
        return m_new, l, acc

    for j in range(n_local):
        qb = qb0 + j
        qrows = q_ref[j * BLK:(j + 1) * BLK, :]
        qs = jnp.concatenate([qrows[:, h * HD:(h + 1) * HD] for h in range(QH)], axis=0)

        block_copy(qb, dbuf.at[j], dsems.at[j]).wait()
        kvd = dbuf[j]
        sc = lax.dot_general(qs, kvd[:, :HD], dims, preferred_element_type=jnp.float32) * scale
        m = jnp.max(jnp.where(causal, sc, masked_score), axis=1, keepdims=True)
        w = jnp.where(causal, jnp.exp(sc - m), 0.0)
        l = jnp.sum(w, axis=1, keepdims=True)
        acc = jnp.dot(w.astype(jnp.bfloat16), kvd[:, HD:], preferred_element_type=jnp.float32)

        def grouped(g, carry, j=j, qs=qs):
            first = g * group
            for i in range(group):
                copy(j, first + i).wait()
            kvb = kvbuf[j, pl.ds(first, group)].reshape(group * BLK, width)
            return update(qs, kvb, carry)

        def single(s, carry, j=j, qs=qs):
            copy(j, s).wait()
            return update(qs, kvbuf[j, s], carry)

        n_groups = n_off[j] // group
        carry = lax.fori_loop(0, n_groups, grouped, (m, l, acc))
        m, l, acc = lax.fori_loop(n_groups * group, n_off[j], single, carry)
        res = (acc / l).astype(out_ref.dtype)
        for h in range(QH):
            out_ref[j * BLK:(j + 1) * BLK, h * HD:(h + 1) * HD] = res[h * BLK:(h + 1) * BLK, :]


def shards(queries, key_cache, value_cache, block_list, block_count, *, n_pb, n_ka):
    kv_local = jnp.concatenate([key_cache, value_cache], axis=1)
    n_half = kv_local.shape[0] // BLK
    kv_pieces = []
    shard = None
    for h in range(n_half):
        part = kv_local[h * BLK:(h + 1) * BLK]
        if shard is not None:
            part, shard = lax.optimization_barrier((part, shard))
            kv_pieces += pieces_axis(shard, "ka", n_ka)
        shard = gather_axis(part, "pb", n_pb)
    kv_pieces += pieces_axis(shard, "ka", n_ka)

    p = lax.axis_index("pb")
    k = lax.axis_index("ka")
    rows_mine = queries.shape[0] // n_ka
    n_local = rows_mine // BLK
    listed = block_list.shape[1]
    q_mine = lax.dynamic_slice_in_dim(queries, k * rows_mine, rows_mine, 0)
    bl_mine = lax.dynamic_slice_in_dim(block_list, k * n_local, n_local, 0)
    cnt_mine = lax.dynamic_slice_in_dim(block_count, k * n_local, n_local, 0)
    qb0 = jnp.stack([(p * n_ka + k) * n_local, k]).astype(jnp.int32)

    kernel = functools.partial(
        attend_kernel, n_local=n_local, n_pieces=len(kv_pieces), n_ka=n_ka, group=4, scale=1.0 / math.sqrt(HD)
    )
    return pl.pallas_call(
        kernel,
        out_shape=jax.ShapeDtypeStruct((rows_mine, queries.shape[1]), jnp.bfloat16),
        grid_spec=pltpu.PrefetchScalarGridSpec(
            num_scalar_prefetch=3,
            grid=(1,),
            in_specs=[
                pl.BlockSpec((rows_mine, queries.shape[1]), lambda i, *_: (0, 0)),
            ]
            + [pl.BlockSpec(memory_space=pl.ANY)] * len(kv_pieces),
            out_specs=pl.BlockSpec((rows_mine, queries.shape[1]), lambda i, *_: (0, 0)),
            scratch_shapes=[
                pltpu.SMEM((n_local, listed), jnp.int32),
                pltpu.VMEM((n_local, listed, BLK, kv_local.shape[1]), jnp.bfloat16),
                pltpu.VMEM((n_local, BLK, kv_local.shape[1]), jnp.bfloat16),
                pltpu.SemaphoreType.DMA((n_local, listed)),
                pltpu.SemaphoreType.DMA((n_local,)),
            ],
        ),
        compiler_params=pltpu.CompilerParams(vmem_limit_bytes=48 * 1024 * 1024),
    )(bl_mine, cnt_mine, qb0, q_mine, *kv_pieces)


def solution(mesh):
    placed = (P("pb", None), P(("ka", "pb"), None), P(("ka", "pb"), None), P("pb", None), P("pb"))
    body = functools.partial(shards, n_pb=mesh.shape["pb"], n_ka=mesh.shape["ka"])
    return jax.shard_map(
        body, mesh=mesh, in_specs=placed, out_specs=P(("pb", "ka"), None), check_vma=False
    )
```

```python
import functools
import math

import jax
import jax.numpy as jnp
from jax import lax
from jax.experimental import pallas as pl
from jax.experimental.pallas import tpu as pltpu
from jax.sharding import PartitionSpec as P

HD = 128
QH = 4
BLK = 128

masked_score = -1e30


def gather_axis(local, axis, n):
    idx = lax.axis_index(axis)
    bits = n.bit_length() - 1
    held = local.reshape((1,) * bits + local.shape)
    for t in range(bits):
        b = n >> (t + 1)
        other = lax.ppermute(held, axis, [(i, i ^ b) for i in range(n)])
        upper = (idx // b) % 2 == 1
        held = jnp.where(
            upper,
            jnp.concatenate([other, held], axis=t),
            jnp.concatenate([held, other], axis=t),
        )
    return held.reshape((n * local.shape[0],) + local.shape[1:])


def pieces_axis(local, axis, n):
    idx_pieces = {0: local}
    b = n // 2
    while b >= 1:
        for x in sorted(idx_pieces):
            idx_pieces[x | b] = lax.ppermute(idx_pieces[x], axis, [(i, i ^ b) for i in range(n)])
        b //= 2
    return [idx_pieces[x] for x in range(n)]


def attend_kernel(bl_ref, cnt_ref, qb_ref, q_ref, *rest, n_local, n_pieces, n_ka, group, scale):
    kv_pieces = rest[:n_pieces]
    out_ref, off_ref, kvbuf, dbuf, sems, dsems = rest[n_pieces:]
    qb0 = qb_ref[0]
    me = qb_ref[1]
    width = kvbuf.shape[-1]
    per_piece = kv_pieces[0].shape[0] // BLK
    n_half = n_pieces // n_ka

    class block_copy:
        def __init__(self, blk, dst, sem):
            self.blk, self.dst, self.sem = blk, dst, sem

        def start(self):
            per_shard = per_piece * n_half
            within = self.blk % per_shard
            which = (within % n_half) * n_ka + jnp.bitwise_xor(self.blk // per_shard, me)
            start = pl.multiple_of((within // n_half) * BLK, BLK)
            for x in range(n_pieces):
                @pl.when(which == x)
                def _(x=x, start=start):
                    pltpu.make_async_copy(kv_pieces[x].at[pl.ds(start, BLK), :], self.dst, self.sem).start()

        def wait(self):
            pltpu.make_async_copy(kv_pieces[0].at[pl.ds(0, BLK), :], self.dst, self.sem).wait()

    def copy(j, s):
        return block_copy(off_ref[j, s], kvbuf.at[j, s], sems.at[j, s])

    n_off = []
    for j in range(n_local):
        qb = qb0 + j
        block_copy(qb, dbuf.at[j], dsems.at[j]).start()

        def compact(s, n, j=j, qb=qb):
            b = bl_ref[j, s]
            off_ref[j, n] = b
            return n + (b != qb).astype(jnp.int32)

        n_j = lax.fori_loop(0, cnt_ref[j], compact, 0)
        n_off.append(n_j)

        def issue(s, c, j=j):
            copy(j, s).start()
            return c

        lax.fori_loop(0, n_j, issue, 0)

    rows = QH * BLK
    rowpos = lax.broadcasted_iota(jnp.int32, (rows, BLK), 0) % BLK
    col = lax.broadcasted_iota(jnp.int32, (rows, BLK), 1)
    causal = col <= rowpos
    dims = (((1,), (1,)), ((), ()))

    def update(qs, kvb, carry):
        m, l, acc = carry
        k = kvb[:, :HD]
        v = kvb[:, HD:]
        sc = lax.dot_general(qs, k, dims, preferred_element_type=jnp.float32) * scale
        m_new = jnp.maximum(m, jnp.max(sc, axis=1, keepdims=True))
        alpha = jnp.exp2(m - m_new)
        w = jnp.exp2(sc - m_new)
        l = alpha * l + jnp.sum(w, axis=1, keepdims=True)
        acc = alpha * acc + jnp.dot(w.astype(jnp.bfloat16), v, preferred_element_type=jnp.float32)
        return m_new, l, acc

    for j in range(n_local):
        qb = qb0 + j
        qrows = q_ref[j * BLK:(j + 1) * BLK, :]
        qs = jnp.concatenate([qrows[:, h * HD:(h + 1) * HD] for h in range(QH)], axis=0)

        block_copy(qb, dbuf.at[j], dsems.at[j]).wait()
        kvd = dbuf[j]
        sc = lax.dot_general(qs, kvd[:, :HD], dims, preferred_element_type=jnp.float32) * scale
        m = jnp.max(jnp.where(causal, sc, masked_score), axis=1, keepdims=True)
        w = jnp.where(causal, jnp.exp2(sc - m), 0.0)
        l = jnp.sum(w, axis=1, keepdims=True)
        acc = jnp.dot(w.astype(jnp.bfloat16), kvd[:, HD:], preferred_element_type=jnp.float32)

        def grouped(g, carry, j=j, qs=qs):
            first = g * group
            for i in range(group):
                copy(j, first + i).wait()
            kvb = kvbuf[j, pl.ds(first, group)].reshape(group * BLK, width)
            return update(qs, kvb, carry)

        def single(s, carry, j=j, qs=qs):
            copy(j, s).wait()
            return update(qs, kvbuf[j, s], carry)

        n_groups = n_off[j] // group
        carry = lax.fori_loop(0, n_groups, grouped, (m, l, acc))
        m, l, acc = lax.fori_loop(n_groups * group, n_off[j], single, carry)
        res = (acc / l).astype(out_ref.dtype)
        for h in range(QH):
            out_ref[j * BLK:(j + 1) * BLK, h * HD:(h + 1) * HD] = res[h * BLK:(h + 1) * BLK, :]


def shards(queries, key_cache, value_cache, block_list, block_count, *, n_pb, n_ka):
    kv_local = jnp.concatenate([key_cache, value_cache], axis=1)
    n_half = kv_local.shape[0] // BLK
    kv_pieces = []
    shard = None
    for h in range(n_half):
        part = kv_local[h * BLK:(h + 1) * BLK]
        if shard is not None:
            part, shard = lax.optimization_barrier((part, shard))
            kv_pieces += pieces_axis(shard, "ka", n_ka)
        shard = gather_axis(part, "pb", n_pb)
    kv_pieces += pieces_axis(shard, "ka", n_ka)

    p = lax.axis_index("pb")
    k = lax.axis_index("ka")
    rows_mine = queries.shape[0] // n_ka
    n_local = rows_mine // BLK
    listed = block_list.shape[1]
    q_mine = lax.dynamic_slice_in_dim(queries, k * rows_mine, rows_mine, 0)
    bl_mine = lax.dynamic_slice_in_dim(block_list, k * n_local, n_local, 0)
    cnt_mine = lax.dynamic_slice_in_dim(block_count, k * n_local, n_local, 0)
    qb0 = jnp.stack([(p * n_ka + k) * n_local, k]).astype(jnp.int32)

    kernel = functools.partial(
        attend_kernel, n_local=n_local, n_pieces=len(kv_pieces), n_ka=n_ka, group=4, scale=math.log2(math.e) / math.sqrt(HD)
    )
    return pl.pallas_call(
        kernel,
        out_shape=jax.ShapeDtypeStruct((rows_mine, queries.shape[1]), jnp.bfloat16),
        grid_spec=pltpu.PrefetchScalarGridSpec(
            num_scalar_prefetch=3,
            grid=(1,),
            in_specs=[
                pl.BlockSpec((rows_mine, queries.shape[1]), lambda i, *_: (0, 0)),
            ]
            + [pl.BlockSpec(memory_space=pl.ANY)] * len(kv_pieces),
            out_specs=pl.BlockSpec((rows_mine, queries.shape[1]), lambda i, *_: (0, 0)),
            scratch_shapes=[
                pltpu.SMEM((n_local, listed), jnp.int32),
                pltpu.VMEM((n_local, listed, BLK, kv_local.shape[1]), jnp.bfloat16),
                pltpu.VMEM((n_local, BLK, kv_local.shape[1]), jnp.bfloat16),
                pltpu.SemaphoreType.DMA((n_local, listed)),
                pltpu.SemaphoreType.DMA((n_local,)),
            ],
        ),
        compiler_params=pltpu.CompilerParams(vmem_limit_bytes=48 * 1024 * 1024),
    )(bl_mine, cnt_mine, qb0, q_mine, *kv_pieces)


def solution(mesh):
    placed = (P("pb", None), P(("ka", "pb"), None), P(("ka", "pb"), None), P("pb", None), P("pb"))
    body = functools.partial(shards, n_pb=mesh.shape["pb"], n_ka=mesh.shape["ka"])
    return jax.shard_map(
        body, mesh=mesh, in_specs=placed, out_specs=P(("pb", "ka"), None), check_vma=False
    )
```

```python
import functools
import math

import jax
import jax.numpy as jnp
from jax import lax
from jax.experimental import pallas as pl
from jax.experimental.pallas import tpu as pltpu
from jax.sharding import PartitionSpec as P

HD = 128
QH = 4
BLK = 128

masked_score = -1e30


def gather_axis(local, axis, n):
    idx = lax.axis_index(axis)
    bits = n.bit_length() - 1
    held = local.reshape((1,) * bits + local.shape)
    for t in range(bits):
        b = n >> (t + 1)
        other = lax.ppermute(held, axis, [(i, i ^ b) for i in range(n)])
        upper = (idx // b) % 2 == 1
        held = jnp.where(
            upper,
            jnp.concatenate([other, held], axis=t),
            jnp.concatenate([held, other], axis=t),
        )
    return held.reshape((n * local.shape[0],) + local.shape[1:])


def pieces_axis(local, axis, n):
    idx_pieces = {0: local}
    b = n // 2
    while b >= 1:
        for x in sorted(idx_pieces):
            idx_pieces[x | b] = lax.ppermute(idx_pieces[x], axis, [(i, i ^ b) for i in range(n)])
        b //= 2
    return [idx_pieces[x] for x in range(n)]


def attend_kernel(bl_ref, cnt_ref, qb_ref, q_ref, *rest, n_local, n_pieces, n_ka, group, scale):
    kv_pieces = rest[:n_pieces]
    out_ref, off_ref, kvbuf, dbuf, sems, dsems = rest[n_pieces:]
    qb0 = qb_ref[0]
    me = qb_ref[1]
    width = kvbuf.shape[-1]
    per_piece = kv_pieces[0].shape[0] // BLK
    n_half = n_pieces // n_ka

    class block_copy:
        def __init__(self, blk, dst, sem):
            self.blk, self.dst, self.sem = blk, dst, sem

        def start(self):
            per_shard = per_piece * n_half
            within = self.blk % per_shard
            which = (within % n_half) * n_ka + jnp.bitwise_xor(self.blk // per_shard, me)
            start = pl.multiple_of((within // n_half) * BLK, BLK)
            for x in range(n_pieces):
                @pl.when(which == x)
                def _(x=x, start=start):
                    pltpu.make_async_copy(kv_pieces[x].at[pl.ds(start, BLK), :], self.dst, self.sem).start()

        def wait(self):
            pltpu.make_async_copy(kv_pieces[0].at[pl.ds(0, BLK), :], self.dst, self.sem).wait()

    def copy(j, s):
        return block_copy(off_ref[j, s], kvbuf.at[j, s], sems.at[j, s])

    n_off = []
    for j in range(n_local):
        qb = qb0 + j
        block_copy(qb, dbuf.at[j], dsems.at[j]).start()

        def compact(s, n, j=j, qb=qb):
            b = bl_ref[j, s]
            off_ref[j, n] = b
            return n + (b != qb).astype(jnp.int32)

        n_j = lax.fori_loop(0, cnt_ref[j], compact, 0)
        n_off.append(n_j)

        def issue(s, c, j=j):
            copy(j, s).start()
            return c

        lax.fori_loop(0, n_j, issue, 0)

    rowpos = lax.broadcasted_iota(jnp.int32, (BLK, BLK), 0)
    col = lax.broadcasted_iota(jnp.int32, (BLK, BLK), 1)
    causal = col <= rowpos
    dims = (((1,), (1,)), ((), ()))

    def update(qh, kvb, carry):
        k = kvb[:, :HD]
        v = kvb[:, HD:]
        out = []
        for h in range(QH):
            m, l, acc = carry[h]
            sc = lax.dot_general(qh[h], k, dims, preferred_element_type=jnp.float32) * scale
            m_new = jnp.maximum(m, jnp.max(sc, axis=1, keepdims=True))
            alpha = jnp.exp2(m - m_new)
            w = jnp.exp2(sc - m_new)
            l = alpha * l + jnp.sum(w, axis=1, keepdims=True)
            acc = alpha * acc + jnp.dot(w.astype(jnp.bfloat16), v, preferred_element_type=jnp.float32)
            out.append((m_new, l, acc))
        return tuple(out)

    for j in range(n_local):
        qb = qb0 + j
        qh = [q_ref[j * BLK:(j + 1) * BLK, h * HD:(h + 1) * HD] for h in range(QH)]

        block_copy(qb, dbuf.at[j], dsems.at[j]).wait()
        kvd = dbuf[j]
        carry = []
        for h in range(QH):
            sc = lax.dot_general(qh[h], kvd[:, :HD], dims, preferred_element_type=jnp.float32) * scale
            m = jnp.max(jnp.where(causal, sc, masked_score), axis=1, keepdims=True)
            w = jnp.where(causal, jnp.exp2(sc - m), 0.0)
            l = jnp.sum(w, axis=1, keepdims=True)
            acc = jnp.dot(w.astype(jnp.bfloat16), kvd[:, HD:], preferred_element_type=jnp.float32)
            carry.append((m, l, acc))
        carry = tuple(carry)

        def grouped(g, carry, j=j, qh=qh):
            first = g * group
            for i in range(group):
                copy(j, first + i).wait()
            kvb = kvbuf[j, pl.ds(first, group)].reshape(group * BLK, width)
            return update(qh, kvb, carry)

        def single(s, carry, j=j, qh=qh):
            copy(j, s).wait()
            return update(qh, kvbuf[j, s], carry)

        n_groups = n_off[j] // group
        carry = lax.fori_loop(0, n_groups, grouped, carry)
        carry = lax.fori_loop(n_groups * group, n_off[j], single, carry)
        for h in range(QH):
            m, l, acc = carry[h]
            out_ref[j * BLK:(j + 1) * BLK, h * HD:(h + 1) * HD] = (acc / l).astype(out_ref.dtype)


def shards(queries, key_cache, value_cache, block_list, block_count, *, n_pb, n_ka):
    kv_local = jnp.concatenate([key_cache, value_cache], axis=1)
    n_half = kv_local.shape[0] // BLK
    kv_pieces = []
    shard = None
    for h in range(n_half):
        part = kv_local[h * BLK:(h + 1) * BLK]
        if shard is not None:
            part, shard = lax.optimization_barrier((part, shard))
            kv_pieces += pieces_axis(shard, "ka", n_ka)
        shard = gather_axis(part, "pb", n_pb)
    kv_pieces += pieces_axis(shard, "ka", n_ka)

    p = lax.axis_index("pb")
    k = lax.axis_index("ka")
    rows_mine = queries.shape[0] // n_ka
    n_local = rows_mine // BLK
    listed = block_list.shape[1]
    q_mine = lax.dynamic_slice_in_dim(queries, k * rows_mine, rows_mine, 0)
    bl_mine = lax.dynamic_slice_in_dim(block_list, k * n_local, n_local, 0)
    cnt_mine = lax.dynamic_slice_in_dim(block_count, k * n_local, n_local, 0)
    qb0 = jnp.stack([(p * n_ka + k) * n_local, k]).astype(jnp.int32)

    kernel = functools.partial(
        attend_kernel, n_local=n_local, n_pieces=len(kv_pieces), n_ka=n_ka, group=4, scale=math.log2(math.e) / math.sqrt(HD)
    )
    return pl.pallas_call(
        kernel,
        out_shape=jax.ShapeDtypeStruct((rows_mine, queries.shape[1]), jnp.bfloat16),
        grid_spec=pltpu.PrefetchScalarGridSpec(
            num_scalar_prefetch=3,
            grid=(1,),
            in_specs=[
                pl.BlockSpec((rows_mine, queries.shape[1]), lambda i, *_: (0, 0)),
            ]
            + [pl.BlockSpec(memory_space=pl.ANY)] * len(kv_pieces),
            out_specs=pl.BlockSpec((rows_mine, queries.shape[1]), lambda i, *_: (0, 0)),
            scratch_shapes=[
                pltpu.SMEM((n_local, listed), jnp.int32),
                pltpu.VMEM((n_local, listed, BLK, kv_local.shape[1]), jnp.bfloat16),
                pltpu.VMEM((n_local, BLK, kv_local.shape[1]), jnp.bfloat16),
                pltpu.SemaphoreType.DMA((n_local, listed)),
                pltpu.SemaphoreType.DMA((n_local,)),
            ],
        ),
        compiler_params=pltpu.CompilerParams(vmem_limit_bytes=48 * 1024 * 1024),
    )(bl_mine, cnt_mine, qb0, q_mine, *kv_pieces)


def solution(mesh):
    placed = (P("pb", None), P(("ka", "pb"), None), P(("ka", "pb"), None), P("pb", None), P("pb"))
    body = functools.partial(shards, n_pb=mesh.shape["pb"], n_ka=mesh.shape["ka"])
    return jax.shard_map(
        body, mesh=mesh, in_specs=placed, out_specs=P(("pb", "ka"), None), check_vma=False
    )
```

```python
import functools
import math

import jax
import jax.numpy as jnp
from jax import lax
from jax.experimental import pallas as pl
from jax.experimental.pallas import tpu as pltpu
from jax.sharding import PartitionSpec as P

HD = 128
QH = 4
BLK = 128

masked_score = -1e30


def gather_axis(local, axis, n):
    idx = lax.axis_index(axis)
    bits = n.bit_length() - 1
    held = local.reshape((1,) * bits + local.shape)
    for t in range(bits):
        b = n >> (t + 1)
        other = lax.ppermute(held, axis, [(i, i ^ b) for i in range(n)])
        upper = (idx // b) % 2 == 1
        held = jnp.where(
            upper,
            jnp.concatenate([other, held], axis=t),
            jnp.concatenate([held, other], axis=t),
        )
    return held.reshape((n * local.shape[0],) + local.shape[1:])


def pieces_axis(local, axis, n):
    idx_pieces = {0: local}
    b = n // 2
    while b >= 1:
        for x in sorted(idx_pieces):
            idx_pieces[x | b] = lax.ppermute(idx_pieces[x], axis, [(i, i ^ b) for i in range(n)])
        b //= 2
    return [idx_pieces[x] for x in range(n)]


def attend_kernel(bl_ref, cnt_ref, qb_ref, q_ref, *rest, n_local, n_pieces, n_ka, group, scale):
    kv_pieces = rest[:n_pieces]
    out_ref, off_ref, kvbuf, dbuf, sems, dsems = rest[n_pieces:]
    qb0 = qb_ref[0]
    me = qb_ref[1]
    width = kvbuf.shape[-1]
    per_piece = kv_pieces[0].shape[0] // BLK
    n_half = n_pieces // n_ka

    class block_copy:
        def __init__(self, blk, dst, sem):
            self.blk, self.dst, self.sem = blk, dst, sem

        def start(self):
            per_shard = per_piece * n_half
            within = self.blk % per_shard
            which = (within % n_half) * n_ka + jnp.bitwise_xor(self.blk // per_shard, me)
            start = pl.multiple_of((within // n_half) * BLK, BLK)
            for x in range(n_pieces):
                @pl.when(which == x)
                def _(x=x, start=start):
                    pltpu.make_async_copy(kv_pieces[x].at[pl.ds(start, BLK), :], self.dst, self.sem).start()

        def wait(self):
            pltpu.make_async_copy(kv_pieces[0].at[pl.ds(0, BLK), :], self.dst, self.sem).wait()

    def copy(j, s):
        return block_copy(off_ref[j, s], kvbuf.at[j, s], sems.at[j, s])

    n_off = []
    for j in range(n_local):
        qb = qb0 + j
        block_copy(qb, dbuf.at[j], dsems.at[j]).start()

        def compact(s, n, j=j, qb=qb):
            b = bl_ref[j, s]
            off_ref[j, n] = b
            return n + (b != qb).astype(jnp.int32)

        n_j = lax.fori_loop(0, cnt_ref[j], compact, 0)
        n_off.append(n_j)
        n_pad = (n_j + group - 1) // group * group

        def pad(s, c, j=j, qb=qb):
            off_ref[j, s] = qb
            return c

        lax.fori_loop(n_j, n_pad, pad, 0)

        def issue(s, c, j=j):
            copy(j, s).start()
            return c

        lax.fori_loop(0, n_pad, issue, 0)

    rows = QH * BLK
    rowpos = lax.broadcasted_iota(jnp.int32, (rows, BLK), 0) % BLK
    col = lax.broadcasted_iota(jnp.int32, (rows, BLK), 1)
    causal = col <= rowpos
    dims = (((1,), (1,)), ((), ()))

    slot_of = lax.broadcasted_iota(jnp.int32, (rows, group * BLK), 1) // BLK

    def update(qs, kvb, carry, live=None):
        m, l, acc = carry
        k = kvb[:, :HD]
        v = kvb[:, HD:]
        sc = lax.dot_general(qs, k, dims, preferred_element_type=jnp.float32) * scale
        if live is not None:
            sc = jnp.where(slot_of < live, sc, masked_score)
        m_new = jnp.maximum(m, jnp.max(sc, axis=1, keepdims=True))
        alpha = jnp.exp2(m - m_new)
        w = jnp.exp2(sc - m_new)
        l = alpha * l + jnp.sum(w, axis=1, keepdims=True)
        acc = alpha * acc + jnp.dot(w.astype(jnp.bfloat16), v, preferred_element_type=jnp.float32)
        return m_new, l, acc

    for j in range(n_local):
        qb = qb0 + j
        qrows = q_ref[j * BLK:(j + 1) * BLK, :]
        qs = jnp.concatenate([qrows[:, h * HD:(h + 1) * HD] for h in range(QH)], axis=0)

        block_copy(qb, dbuf.at[j], dsems.at[j]).wait()
        kvd = dbuf[j]
        sc = lax.dot_general(qs, kvd[:, :HD], dims, preferred_element_type=jnp.float32) * scale
        m = jnp.max(jnp.where(causal, sc, masked_score), axis=1, keepdims=True)
        w = jnp.where(causal, jnp.exp2(sc - m), 0.0)
        l = jnp.sum(w, axis=1, keepdims=True)
        acc = jnp.dot(w.astype(jnp.bfloat16), kvd[:, HD:], preferred_element_type=jnp.float32)

        def grouped(g, carry, j=j, qs=qs):
            first = g * group
            for i in range(group):
                copy(j, first + i).wait()
            kvb = kvbuf[j, pl.ds(first, group)].reshape(group * BLK, width)
            return update(qs, kvb, carry)

        def last(g, carry, j=j, qs=qs):
            first = g * group
            for i in range(group):
                copy(j, first + i).wait()
            kvb = kvbuf[j, pl.ds(first, group)].reshape(group * BLK, width)
            return update(qs, kvb, carry, live=n_off[j] - first)

        n_groups = n_off[j] // group
        carry = lax.fori_loop(0, n_groups, grouped, (m, l, acc))
        m, l, acc = lax.fori_loop(n_groups, (n_off[j] + group - 1) // group, last, carry)
        res = (acc / l).astype(out_ref.dtype)
        for h in range(QH):
            out_ref[j * BLK:(j + 1) * BLK, h * HD:(h + 1) * HD] = res[h * BLK:(h + 1) * BLK, :]


def shards(queries, key_cache, value_cache, block_list, block_count, *, n_pb, n_ka):
    kv_local = jnp.concatenate([key_cache, value_cache], axis=1)
    n_half = kv_local.shape[0] // BLK
    kv_pieces = []
    shard = None
    for h in range(n_half):
        part = kv_local[h * BLK:(h + 1) * BLK]
        if shard is not None:
            part, shard = lax.optimization_barrier((part, shard))
            kv_pieces += pieces_axis(shard, "ka", n_ka)
        shard = gather_axis(part, "pb", n_pb)
    kv_pieces += pieces_axis(shard, "ka", n_ka)

    p = lax.axis_index("pb")
    k = lax.axis_index("ka")
    rows_mine = queries.shape[0] // n_ka
    n_local = rows_mine // BLK
    listed = block_list.shape[1]
    q_mine = lax.dynamic_slice_in_dim(queries, k * rows_mine, rows_mine, 0)
    bl_mine = lax.dynamic_slice_in_dim(block_list, k * n_local, n_local, 0)
    cnt_mine = lax.dynamic_slice_in_dim(block_count, k * n_local, n_local, 0)
    qb0 = jnp.stack([(p * n_ka + k) * n_local, k]).astype(jnp.int32)

    kernel = functools.partial(
        attend_kernel, n_local=n_local, n_pieces=len(kv_pieces), n_ka=n_ka, group=8, scale=math.log2(math.e) / math.sqrt(HD)
    )
    return pl.pallas_call(
        kernel,
        out_shape=jax.ShapeDtypeStruct((rows_mine, queries.shape[1]), jnp.bfloat16),
        grid_spec=pltpu.PrefetchScalarGridSpec(
            num_scalar_prefetch=3,
            grid=(1,),
            in_specs=[
                pl.BlockSpec((rows_mine, queries.shape[1]), lambda i, *_: (0, 0)),
            ]
            + [pl.BlockSpec(memory_space=pl.ANY)] * len(kv_pieces),
            out_specs=pl.BlockSpec((rows_mine, queries.shape[1]), lambda i, *_: (0, 0)),
            scratch_shapes=[
                pltpu.SMEM((n_local, listed), jnp.int32),
                pltpu.VMEM((n_local, listed, BLK, kv_local.shape[1]), jnp.bfloat16),
                pltpu.VMEM((n_local, BLK, kv_local.shape[1]), jnp.bfloat16),
                pltpu.SemaphoreType.DMA((n_local, listed)),
                pltpu.SemaphoreType.DMA((n_local,)),
            ],
        ),
        compiler_params=pltpu.CompilerParams(vmem_limit_bytes=48 * 1024 * 1024),
    )(bl_mine, cnt_mine, qb0, q_mine, *kv_pieces)


def solution(mesh):
    placed = (P("pb", None), P(("ka", "pb"), None), P(("ka", "pb"), None), P("pb", None), P("pb"))
    body = functools.partial(shards, n_pb=mesh.shape["pb"], n_ka=mesh.shape["ka"])
    return jax.shard_map(
        body, mesh=mesh, in_specs=placed, out_specs=P(("pb", "ka"), None), check_vma=False
    )
```

```python
import functools
import math

import jax
import jax.numpy as jnp
from jax import lax
from jax.experimental import pallas as pl
from jax.experimental.pallas import tpu as pltpu
from jax.sharding import PartitionSpec as P

HD = 128
QH = 4
BLK = 128

masked_score = -1e30


def gather_axis(local, axis, n):
    idx = lax.axis_index(axis)
    bits = n.bit_length() - 1
    held = local.reshape((1,) * bits + local.shape)
    for t in range(bits):
        b = n >> (t + 1)
        other = lax.ppermute(held, axis, [(i, i ^ b) for i in range(n)])
        upper = (idx // b) % 2 == 1
        held = jnp.where(
            upper,
            jnp.concatenate([other, held], axis=t),
            jnp.concatenate([held, other], axis=t),
        )
    return held.reshape((n * local.shape[0],) + local.shape[1:])


def pieces_axis(local, axis, n):
    idx_pieces = {0: local}
    b = n // 2
    while b >= 1:
        for x in sorted(idx_pieces):
            idx_pieces[x | b] = lax.ppermute(idx_pieces[x], axis, [(i, i ^ b) for i in range(n)])
        b //= 2
    return [idx_pieces[x] for x in range(n)]


def attend_kernel(bl_ref, cnt_ref, qb_ref, q_ref, *rest, n_local, n_pieces, n_ka, group, scale):
    kv_pieces = rest[:n_pieces]
    out_ref, off_ref, kvbuf, dbuf, sems, dsems = rest[n_pieces:]
    qb0 = qb_ref[0]
    me = qb_ref[1]
    width = kvbuf.shape[-1]
    per_piece = kv_pieces[0].shape[0] // BLK
    n_half = n_pieces // n_ka

    class block_copy:
        def __init__(self, blk, dst, sem):
            self.blk, self.dst, self.sem = blk, dst, sem

        def start(self):
            per_shard = per_piece * n_half
            within = self.blk % per_shard
            which = (within % n_half) * n_ka + jnp.bitwise_xor(self.blk // per_shard, me)
            start = pl.multiple_of((within // n_half) * BLK, BLK)
            for x in range(n_pieces):
                @pl.when(which == x)
                def _(x=x, start=start):
                    pltpu.make_async_copy(kv_pieces[x].at[pl.ds(start, BLK), :], self.dst, self.sem).start()

        def wait(self):
            pltpu.make_async_copy(kv_pieces[0].at[pl.ds(0, BLK), :], self.dst, self.sem).wait()

    def copy(j, s):
        return block_copy(off_ref[j, s], kvbuf.at[j, s], sems.at[j, s])

    n_off = []
    for j in range(n_local):
        qb = qb0 + j
        block_copy(qb, dbuf.at[j], dsems.at[j]).start()

        def compact(s, n, j=j, qb=qb):
            b = bl_ref[j, s]
            off_ref[j, n] = b
            return n + (b != qb).astype(jnp.int32)

        n_j = lax.fori_loop(0, cnt_ref[j], compact, 0)
        n_off.append(n_j)
        n_pad = (n_j + group - 1) // group * group

        def pad(s, c, j=j, qb=qb):
            off_ref[j, s] = qb
            return c

        lax.fori_loop(n_j, n_pad, pad, 0)

        def issue(s, c, j=j):
            copy(j, s).start()
            return c

        lax.fori_loop(0, n_pad, issue, 0)

    rows = QH * BLK
    rowpos = lax.broadcasted_iota(jnp.int32, (rows, BLK), 0) % BLK
    col = lax.broadcasted_iota(jnp.int32, (rows, BLK), 1)
    causal = col <= rowpos
    dims = (((1,), (1,)), ((), ()))

    slot_of = lax.broadcasted_iota(jnp.int32, (rows, group * BLK), 1) // BLK

    def update(qs, kvb, carry, live=None):
        m, l, acc = carry
        k = kvb[:, :HD]
        v = kvb[:, HD:]
        sc = lax.dot_general(qs, k, dims, preferred_element_type=jnp.float32) * scale
        if live is not None:
            sc = jnp.where(slot_of < live, sc, masked_score)
        m_new = jnp.maximum(m, jnp.max(sc, axis=1, keepdims=True))
        alpha = jnp.exp2(m - m_new)
        w = jnp.exp2(sc - m_new)
        l = alpha * l + jnp.sum(w, axis=1, keepdims=True)
        acc = alpha * acc + jnp.dot(w.astype(jnp.bfloat16), v, preferred_element_type=jnp.float32)
        return m_new, l, acc

    for j in range(n_local):
        qb = qb0 + j
        qrows = q_ref[j * BLK:(j + 1) * BLK, :]
        qs = jnp.concatenate([qrows[:, h * HD:(h + 1) * HD] for h in range(QH)], axis=0)

        block_copy(qb, dbuf.at[j], dsems.at[j]).wait()
        kvd = dbuf[j]
        sc = lax.dot_general(qs, kvd[:, :HD], dims, preferred_element_type=jnp.float32) * scale
        m = jnp.max(jnp.where(causal, sc, masked_score), axis=1, keepdims=True)
        w = jnp.where(causal, jnp.exp2(sc - m), 0.0)
        l = jnp.sum(w, axis=1, keepdims=True)
        acc = jnp.dot(w.astype(jnp.bfloat16), kvd[:, HD:], preferred_element_type=jnp.float32)

        def grouped(g, carry, j=j, qs=qs):
            first = g * group
            for i in range(group):
                copy(j, first + i).wait()
            kvb = kvbuf[j, pl.ds(first, group)].reshape(group * BLK, width)
            return update(qs, kvb, carry)

        def last(g, carry, j=j, qs=qs):
            first = g * group
            for i in range(group):
                copy(j, first + i).wait()
            kvb = kvbuf[j, pl.ds(first, group)].reshape(group * BLK, width)
            return update(qs, kvb, carry, live=n_off[j] - first)

        n_groups = n_off[j] // group
        carry = lax.fori_loop(0, n_groups, grouped, (m, l, acc))
        m, l, acc = lax.fori_loop(n_groups, (n_off[j] + group - 1) // group, last, carry)
        res = (acc / l).astype(out_ref.dtype)
        for h in range(QH):
            out_ref[j * BLK:(j + 1) * BLK, h * HD:(h + 1) * HD] = res[h * BLK:(h + 1) * BLK, :]


def shards(queries, key_cache, value_cache, block_list, block_count, *, n_pb, n_ka):
    kv_local = jnp.concatenate([key_cache, value_cache], axis=1)
    n_half = kv_local.shape[0] // BLK
    kv_pieces = []
    shard = None
    for h in range(n_half):
        part = kv_local[h * BLK:(h + 1) * BLK]
        if shard is not None:
            part, shard = lax.optimization_barrier((part, shard))
            kv_pieces += pieces_axis(shard, "ka", n_ka)
        shard = gather_axis(part, "pb", n_pb)
    kv_pieces += pieces_axis(shard, "ka", n_ka)

    p = lax.axis_index("pb")
    k = lax.axis_index("ka")
    rows_mine = queries.shape[0] // n_ka
    n_local = rows_mine // BLK
    listed = block_list.shape[1]
    q_mine = lax.dynamic_slice_in_dim(queries, k * rows_mine, rows_mine, 0)
    bl_mine = lax.dynamic_slice_in_dim(block_list, k * n_local, n_local, 0)
    cnt_mine = lax.dynamic_slice_in_dim(block_count, k * n_local, n_local, 0)
    qb0 = jnp.stack([(p * n_ka + k) * n_local, k]).astype(jnp.int32)

    kernel = functools.partial(
        attend_kernel, n_local=n_local, n_pieces=len(kv_pieces), n_ka=n_ka, group=16, scale=math.log2(math.e) / math.sqrt(HD)
    )
    return pl.pallas_call(
        kernel,
        out_shape=jax.ShapeDtypeStruct((rows_mine, queries.shape[1]), jnp.bfloat16),
        grid_spec=pltpu.PrefetchScalarGridSpec(
            num_scalar_prefetch=3,
            grid=(1,),
            in_specs=[
                pl.BlockSpec((rows_mine, queries.shape[1]), lambda i, *_: (0, 0)),
            ]
            + [pl.BlockSpec(memory_space=pl.ANY)] * len(kv_pieces),
            out_specs=pl.BlockSpec((rows_mine, queries.shape[1]), lambda i, *_: (0, 0)),
            scratch_shapes=[
                pltpu.SMEM((n_local, listed), jnp.int32),
                pltpu.VMEM((n_local, listed, BLK, kv_local.shape[1]), jnp.bfloat16),
                pltpu.VMEM((n_local, BLK, kv_local.shape[1]), jnp.bfloat16),
                pltpu.SemaphoreType.DMA((n_local, listed)),
                pltpu.SemaphoreType.DMA((n_local,)),
            ],
        ),
        compiler_params=pltpu.CompilerParams(vmem_limit_bytes=48 * 1024 * 1024),
    )(bl_mine, cnt_mine, qb0, q_mine, *kv_pieces)


def solution(mesh):
    placed = (P("pb", None), P(("ka", "pb"), None), P(("ka", "pb"), None), P("pb", None), P("pb"))
    body = functools.partial(shards, n_pb=mesh.shape["pb"], n_ka=mesh.shape["ka"])
    return jax.shard_map(
        body, mesh=mesh, in_specs=placed, out_specs=P(("pb", "ka"), None), check_vma=False
    )
```

```python
import functools
import math

import jax
import jax.numpy as jnp
from jax import lax
from jax.experimental import pallas as pl
from jax.experimental.pallas import tpu as pltpu
from jax.sharding import PartitionSpec as P

HD = 128
QH = 4
BLK = 128

masked_score = -1e30


def gather_axis(local, axis, n):
    idx = lax.axis_index(axis)
    bits = n.bit_length() - 1
    held = local.reshape((1,) * bits + local.shape)
    for t in range(bits):
        b = n >> (t + 1)
        other = lax.ppermute(held, axis, [(i, i ^ b) for i in range(n)])
        upper = (idx // b) % 2 == 1
        held = jnp.where(
            upper,
            jnp.concatenate([other, held], axis=t),
            jnp.concatenate([held, other], axis=t),
        )
    return held.reshape((n * local.shape[0],) + local.shape[1:])


def pieces_axis(local, axis, n):
    idx_pieces = {0: local}
    b = n // 2
    while b >= 1:
        for x in sorted(idx_pieces):
            idx_pieces[x | b] = lax.ppermute(idx_pieces[x], axis, [(i, i ^ b) for i in range(n)])
        b //= 2
    return [idx_pieces[x] for x in range(n)]


def attend_kernel(bl_ref, cnt_ref, qb_ref, q_ref, *rest, n_local, n_pieces, n_ka, group, scale):
    kv_pieces = rest[:n_pieces]
    out_ref, off_ref, kvbuf, dbuf, sems, dsems = rest[n_pieces:]
    qb0 = qb_ref[0]
    me = qb_ref[1]
    width = kvbuf.shape[-1]
    per_piece = kv_pieces[0].shape[0] // BLK
    n_half = n_pieces // n_ka

    class block_copy:
        def __init__(self, blk, dst, sem):
            self.blk, self.dst, self.sem = blk, dst, sem

        def start(self):
            per_shard = per_piece * n_half
            within = self.blk % per_shard
            which = (within % n_half) * n_ka + jnp.bitwise_xor(self.blk // per_shard, me)
            start = pl.multiple_of((within // n_half) * BLK, BLK)
            for x in range(n_pieces):
                @pl.when(which == x)
                def _(x=x, start=start):
                    pltpu.make_async_copy(kv_pieces[x].at[pl.ds(start, BLK), :], self.dst, self.sem).start()

        def wait(self):
            pltpu.make_async_copy(kv_pieces[0].at[pl.ds(0, BLK), :], self.dst, self.sem).wait()

    def copy(j, s):
        return block_copy(off_ref[j, s], kvbuf.at[j, s, :, pl.ds(0, 2 * HD)], sems.at[j, s])

    kvbuf[:, :, :, 2 * HD:] = jnp.ones(kvbuf.shape[:3] + (HD,), kvbuf.dtype)

    n_off = []
    for j in range(n_local):
        qb = qb0 + j
        block_copy(qb, dbuf.at[j], dsems.at[j]).start()

        def compact(s, n, j=j, qb=qb):
            b = bl_ref[j, s]
            off_ref[j, n] = b
            return n + (b != qb).astype(jnp.int32)

        n_j = lax.fori_loop(0, cnt_ref[j], compact, 0)
        n_off.append(n_j)
        n_pad = (n_j + group - 1) // group * group

        def pad(s, c, j=j, qb=qb):
            off_ref[j, s] = qb
            return c

        lax.fori_loop(n_j, n_pad, pad, 0)

        def issue(s, c, j=j):
            copy(j, s).start()
            return c

        lax.fori_loop(0, n_pad, issue, 0)

    rows = QH * BLK
    rowpos = lax.broadcasted_iota(jnp.int32, (rows, BLK), 0) % BLK
    col = lax.broadcasted_iota(jnp.int32, (rows, BLK), 1)
    causal = col <= rowpos
    dims = (((1,), (1,)), ((), ()))

    slot_of = lax.broadcasted_iota(jnp.int32, (rows, group * BLK), 1) // BLK

    def update(qs, kvb, carry, live=None):
        m, l, acc = carry
        k = kvb[:, :HD]
        v = kvb[:, HD:]
        sc = lax.dot_general(qs, k, dims, preferred_element_type=jnp.float32) * scale
        if live is not None:
            sc = jnp.where(slot_of < live, sc, masked_score)
        m_new = jnp.maximum(m, jnp.max(sc, axis=1, keepdims=True))
        alpha = jnp.exp2(m - m_new)
        w = jnp.exp2(sc - m_new)
        both = jnp.dot(w.astype(jnp.bfloat16), v, preferred_element_type=jnp.float32)
        l = alpha * l + both[:, HD:HD + 1]
        acc = alpha * acc + both[:, :HD]
        return m_new, l, acc

    for j in range(n_local):
        qb = qb0 + j
        qrows = q_ref[j * BLK:(j + 1) * BLK, :]
        qs = jnp.concatenate([qrows[:, h * HD:(h + 1) * HD] for h in range(QH)], axis=0)

        block_copy(qb, dbuf.at[j], dsems.at[j]).wait()
        kvd = dbuf[j]
        sc = lax.dot_general(qs, kvd[:, :HD], dims, preferred_element_type=jnp.float32) * scale
        m = jnp.max(jnp.where(causal, sc, masked_score), axis=1, keepdims=True)
        w = jnp.where(causal, jnp.exp2(sc - m), 0.0)
        l = jnp.sum(w, axis=1, keepdims=True)
        acc = jnp.dot(w.astype(jnp.bfloat16), kvd[:, HD:2 * HD], preferred_element_type=jnp.float32)

        def grouped(g, carry, j=j, qs=qs):
            first = g * group
            for i in range(group):
                copy(j, first + i).wait()
            kvb = kvbuf[j, pl.ds(first, group)].reshape(group * BLK, width)
            return update(qs, kvb, carry)

        def last(g, carry, j=j, qs=qs):
            first = g * group
            for i in range(group):
                copy(j, first + i).wait()
            kvb = kvbuf[j, pl.ds(first, group)].reshape(group * BLK, width)
            return update(qs, kvb, carry, live=n_off[j] - first)

        n_groups = n_off[j] // group
        carry = lax.fori_loop(0, n_groups, grouped, (m, l, acc))
        m, l, acc = lax.fori_loop(n_groups, (n_off[j] + group - 1) // group, last, carry)
        res = (acc / l).astype(out_ref.dtype)
        for h in range(QH):
            out_ref[j * BLK:(j + 1) * BLK, h * HD:(h + 1) * HD] = res[h * BLK:(h + 1) * BLK, :]


def shards(queries, key_cache, value_cache, block_list, block_count, *, n_pb, n_ka):
    kv_local = jnp.concatenate([key_cache, value_cache], axis=1)
    n_half = kv_local.shape[0] // BLK
    kv_pieces = []
    shard = None
    for h in range(n_half):
        part = kv_local[h * BLK:(h + 1) * BLK]
        if shard is not None:
            part, shard = lax.optimization_barrier((part, shard))
            kv_pieces += pieces_axis(shard, "ka", n_ka)
        shard = gather_axis(part, "pb", n_pb)
    kv_pieces += pieces_axis(shard, "ka", n_ka)

    p = lax.axis_index("pb")
    k = lax.axis_index("ka")
    rows_mine = queries.shape[0] // n_ka
    n_local = rows_mine // BLK
    listed = block_list.shape[1]
    q_mine = lax.dynamic_slice_in_dim(queries, k * rows_mine, rows_mine, 0)
    bl_mine = lax.dynamic_slice_in_dim(block_list, k * n_local, n_local, 0)
    cnt_mine = lax.dynamic_slice_in_dim(block_count, k * n_local, n_local, 0)
    qb0 = jnp.stack([(p * n_ka + k) * n_local, k]).astype(jnp.int32)

    kernel = functools.partial(
        attend_kernel, n_local=n_local, n_pieces=len(kv_pieces), n_ka=n_ka, group=16, scale=math.log2(math.e) / math.sqrt(HD)
    )
    return pl.pallas_call(
        kernel,
        out_shape=jax.ShapeDtypeStruct((rows_mine, queries.shape[1]), jnp.bfloat16),
        grid_spec=pltpu.PrefetchScalarGridSpec(
            num_scalar_prefetch=3,
            grid=(1,),
            in_specs=[
                pl.BlockSpec((rows_mine, queries.shape[1]), lambda i, *_: (0, 0)),
            ]
            + [pl.BlockSpec(memory_space=pl.ANY)] * len(kv_pieces),
            out_specs=pl.BlockSpec((rows_mine, queries.shape[1]), lambda i, *_: (0, 0)),
            scratch_shapes=[
                pltpu.SMEM((n_local, listed), jnp.int32),
                pltpu.VMEM((n_local, listed, BLK, kv_local.shape[1] + HD), jnp.bfloat16),
                pltpu.VMEM((n_local, BLK, kv_local.shape[1]), jnp.bfloat16),
                pltpu.SemaphoreType.DMA((n_local, listed)),
                pltpu.SemaphoreType.DMA((n_local,)),
            ],
        ),
        compiler_params=pltpu.CompilerParams(vmem_limit_bytes=48 * 1024 * 1024),
    )(bl_mine, cnt_mine, qb0, q_mine, *kv_pieces)


def solution(mesh):
    placed = (P("pb", None), P(("ka", "pb"), None), P(("ka", "pb"), None), P("pb", None), P("pb"))
    body = functools.partial(shards, n_pb=mesh.shape["pb"], n_ka=mesh.shape["ka"])
    return jax.shard_map(
        body, mesh=mesh, in_specs=placed, out_specs=P(("pb", "ka"), None), check_vma=False
    )
```

```python
import functools
import math

import jax
import jax.numpy as jnp
from jax import lax
from jax.experimental import pallas as pl
from jax.experimental.pallas import tpu as pltpu
from jax.sharding import PartitionSpec as P

HD = 128
QH = 4
BLK = 128

masked_score = -1e30


def gather_axis(local, axis, n):
    idx = lax.axis_index(axis)
    bits = n.bit_length() - 1
    held = local.reshape((1,) * bits + local.shape)
    for t in range(bits):
        b = n >> (t + 1)
        other = lax.ppermute(held, axis, [(i, i ^ b) for i in range(n)])
        upper = (idx // b) % 2 == 1
        held = jnp.where(
            upper,
            jnp.concatenate([other, held], axis=t),
            jnp.concatenate([held, other], axis=t),
        )
    return held.reshape((n * local.shape[0],) + local.shape[1:])


def pieces_axis(local, axis, n):
    idx_pieces = {0: local}
    b = n // 2
    while b >= 1:
        for x in sorted(idx_pieces):
            idx_pieces[x | b] = lax.ppermute(idx_pieces[x], axis, [(i, i ^ b) for i in range(n)])
        b //= 2
    return [idx_pieces[x] for x in range(n)]


def attend_kernel(bl_ref, cnt_ref, qb_ref, q_ref, *rest, n_local, n_pieces, n_ka, group, scale):
    kv_pieces = rest[:n_pieces]
    out_ref, off_ref, kvbuf, dbuf, sems, dsems = rest[n_pieces:]
    qb0 = qb_ref[0]
    me = qb_ref[1]
    width = kvbuf.shape[-1]
    per_piece = kv_pieces[0].shape[0] // BLK
    n_half = n_pieces // n_ka

    class block_copy:
        def __init__(self, blk, dst, sem):
            self.blk, self.dst, self.sem = blk, dst, sem

        def start(self):
            per_shard = per_piece * n_half
            within = self.blk % per_shard
            which = (within % n_half) * n_ka + jnp.bitwise_xor(self.blk // per_shard, me)
            start = pl.multiple_of((within // n_half) * BLK, BLK)
            for x in range(n_pieces):
                @pl.when(which == x)
                def _(x=x, start=start):
                    pltpu.make_async_copy(kv_pieces[x].at[pl.ds(start, BLK), :], self.dst, self.sem).start()

        def wait(self):
            pltpu.make_async_copy(kv_pieces[0].at[pl.ds(0, BLK), :], self.dst, self.sem).wait()

    def copy(j, s):
        return block_copy(off_ref[j, s], kvbuf.at[j, s, :, pl.ds(0, 2 * HD)], sems.at[j, s])

    kvbuf[:, :, :, 2 * HD:] = jnp.ones(kvbuf.shape[:3] + (HD,), kvbuf.dtype)

    n_off = []
    for j in range(n_local):
        qb = qb0 + j
        block_copy(qb, dbuf.at[j], dsems.at[j]).start()

        def compact(s, n, j=j, qb=qb):
            b = bl_ref[j, s]
            off_ref[j, n] = b
            return n + (b != qb).astype(jnp.int32)

        n_j = lax.fori_loop(0, cnt_ref[j], compact, 0)
        n_off.append(n_j)
        n_pad = (n_j + group - 1) // group * group

        def pad(s, c, j=j, qb=qb):
            off_ref[j, s] = qb
            return c

        lax.fori_loop(n_j, n_pad, pad, 0)

        def issue(s, c, j=j):
            copy(j, s).start()
            return c

        lax.fori_loop(0, n_pad, issue, 0)

    rows = QH * BLK
    rowpos = lax.broadcasted_iota(jnp.int32, (rows, BLK), 0) % BLK
    col = lax.broadcasted_iota(jnp.int32, (rows, BLK), 1)
    causal = col <= rowpos
    dims = (((1,), (1,)), ((), ()))

    slot_of = lax.broadcasted_iota(jnp.int32, (rows, group * BLK), 1) // BLK

    def update(qs, kvb, carry, live=None):
        m, l, acc = carry
        k = kvb[:, :HD]
        v = kvb[:, HD:]
        sc = lax.dot_general(qs, k, dims, preferred_element_type=jnp.float32)
        if live is not None:
            sc = jnp.where(slot_of < live, sc, masked_score)
        m_new = jnp.maximum(m, jnp.max(sc, axis=1, keepdims=True) * scale)
        alpha = jnp.exp2(m - m_new)
        w = jnp.exp2(sc * scale - m_new)
        both = jnp.dot(w.astype(jnp.bfloat16), v, preferred_element_type=jnp.float32)
        l = alpha * l + both[:, HD:HD + 1]
        acc = alpha * acc + both[:, :HD]
        return m_new, l, acc

    for j in range(n_local):
        qb = qb0 + j
        qrows = q_ref[j * BLK:(j + 1) * BLK, :]
        qs = jnp.concatenate([qrows[:, h * HD:(h + 1) * HD] for h in range(QH)], axis=0)

        block_copy(qb, dbuf.at[j], dsems.at[j]).wait()
        kvd = dbuf[j]
        sc = lax.dot_general(qs, kvd[:, :HD], dims, preferred_element_type=jnp.float32) * scale
        m = jnp.max(jnp.where(causal, sc, masked_score), axis=1, keepdims=True)
        w = jnp.where(causal, jnp.exp2(sc - m), 0.0)
        l = jnp.sum(w, axis=1, keepdims=True)
        acc = jnp.dot(w.astype(jnp.bfloat16), kvd[:, HD:2 * HD], preferred_element_type=jnp.float32)

        def grouped(g, carry, j=j, qs=qs):
            first = g * group
            for i in range(group):
                copy(j, first + i).wait()
            kvb = kvbuf[j, pl.ds(first, group)].reshape(group * BLK, width)
            return update(qs, kvb, carry)

        def last(g, carry, j=j, qs=qs):
            first = g * group
            for i in range(group):
                copy(j, first + i).wait()
            kvb = kvbuf[j, pl.ds(first, group)].reshape(group * BLK, width)
            return update(qs, kvb, carry, live=n_off[j] - first)

        n_groups = n_off[j] // group
        carry = lax.fori_loop(0, n_groups, grouped, (m, l, acc))
        m, l, acc = lax.fori_loop(n_groups, (n_off[j] + group - 1) // group, last, carry)
        res = (acc / l).astype(out_ref.dtype)
        for h in range(QH):
            out_ref[j * BLK:(j + 1) * BLK, h * HD:(h + 1) * HD] = res[h * BLK:(h + 1) * BLK, :]


def shards(queries, key_cache, value_cache, block_list, block_count, *, n_pb, n_ka):
    kv_local = jnp.concatenate([key_cache, value_cache], axis=1)
    n_half = kv_local.shape[0] // BLK
    kv_pieces = []
    shard = None
    for h in range(n_half):
        part = kv_local[h * BLK:(h + 1) * BLK]
        if shard is not None:
            part, shard = lax.optimization_barrier((part, shard))
            kv_pieces += pieces_axis(shard, "ka", n_ka)
        shard = gather_axis(part, "pb", n_pb)
    kv_pieces += pieces_axis(shard, "ka", n_ka)

    p = lax.axis_index("pb")
    k = lax.axis_index("ka")
    rows_mine = queries.shape[0] // n_ka
    n_local = rows_mine // BLK
    listed = block_list.shape[1]
    q_mine = lax.dynamic_slice_in_dim(queries, k * rows_mine, rows_mine, 0)
    bl_mine = lax.dynamic_slice_in_dim(block_list, k * n_local, n_local, 0)
    cnt_mine = lax.dynamic_slice_in_dim(block_count, k * n_local, n_local, 0)
    qb0 = jnp.stack([(p * n_ka + k) * n_local, k]).astype(jnp.int32)

    kernel = functools.partial(
        attend_kernel, n_local=n_local, n_pieces=len(kv_pieces), n_ka=n_ka, group=16, scale=math.log2(math.e) / math.sqrt(HD)
    )
    return pl.pallas_call(
        kernel,
        out_shape=jax.ShapeDtypeStruct((rows_mine, queries.shape[1]), jnp.bfloat16),
        grid_spec=pltpu.PrefetchScalarGridSpec(
            num_scalar_prefetch=3,
            grid=(1,),
            in_specs=[
                pl.BlockSpec((rows_mine, queries.shape[1]), lambda i, *_: (0, 0)),
            ]
            + [pl.BlockSpec(memory_space=pl.ANY)] * len(kv_pieces),
            out_specs=pl.BlockSpec((rows_mine, queries.shape[1]), lambda i, *_: (0, 0)),
            scratch_shapes=[
                pltpu.SMEM((n_local, listed), jnp.int32),
                pltpu.VMEM((n_local, listed, BLK, kv_local.shape[1] + HD), jnp.bfloat16),
                pltpu.VMEM((n_local, BLK, kv_local.shape[1]), jnp.bfloat16),
                pltpu.SemaphoreType.DMA((n_local, listed)),
                pltpu.SemaphoreType.DMA((n_local,)),
            ],
        ),
        compiler_params=pltpu.CompilerParams(vmem_limit_bytes=48 * 1024 * 1024),
    )(bl_mine, cnt_mine, qb0, q_mine, *kv_pieces)


def solution(mesh):
    placed = (P("pb", None), P(("ka", "pb"), None), P(("ka", "pb"), None), P("pb", None), P("pb"))
    body = functools.partial(shards, n_pb=mesh.shape["pb"], n_ka=mesh.shape["ka"])
    return jax.shard_map(
        body, mesh=mesh, in_specs=placed, out_specs=P(("pb", "ka"), None), check_vma=False
    )
```

```python
import functools
import math

import jax
import jax.numpy as jnp
from jax import lax
from jax.experimental import pallas as pl
from jax.experimental.pallas import tpu as pltpu
from jax.sharding import PartitionSpec as P

HD = 128
QH = 4
BLK = 128

masked_score = -1e30


def gather_axis(local, axis, n):
    idx = lax.axis_index(axis)
    bits = n.bit_length() - 1
    held = local.reshape((1,) * bits + local.shape)
    for t in range(bits):
        b = n >> (t + 1)
        other = lax.ppermute(held, axis, [(i, i ^ b) for i in range(n)])
        upper = (idx // b) % 2 == 1
        held = jnp.where(
            upper,
            jnp.concatenate([other, held], axis=t),
            jnp.concatenate([held, other], axis=t),
        )
    return held.reshape((n * local.shape[0],) + local.shape[1:])


def pieces_axis(local, axis, n):
    idx_pieces = {0: local}
    b = n // 2
    while b >= 1:
        for x in sorted(idx_pieces):
            idx_pieces[x | b] = lax.ppermute(idx_pieces[x], axis, [(i, i ^ b) for i in range(n)])
        b //= 2
    return [idx_pieces[x] for x in range(n)]


def attend_kernel(bl_ref, cnt_ref, qb_ref, q_ref, *rest, n_local, n_pieces, n_ka, group, scale):
    kv_pieces = rest[:n_pieces]
    out_ref, off_ref, kvbuf, dbuf, sems, dsems = rest[n_pieces:]
    qb0 = qb_ref[0]
    me = qb_ref[1]
    width = kvbuf.shape[-1]
    per_piece = kv_pieces[0].shape[0] // BLK
    n_half = n_pieces // n_ka

    class block_copy:
        def __init__(self, blk, dst, sem):
            self.blk, self.dst, self.sem = blk, dst, sem

        def start(self):
            per_shard = per_piece * n_half
            within = self.blk % per_shard
            which = (within % n_half) * n_ka + jnp.bitwise_xor(self.blk // per_shard, me)
            start = pl.multiple_of((within // n_half) * BLK, BLK)
            for x in range(n_pieces):
                @pl.when(which == x)
                def _(x=x, start=start):
                    pltpu.make_async_copy(kv_pieces[x].at[pl.ds(start, BLK), :], self.dst, self.sem).start()

        def wait(self):
            pltpu.make_async_copy(kv_pieces[0].at[pl.ds(0, BLK), :], self.dst, self.sem).wait()

    def copy(j, s):
        return block_copy(off_ref[j, s], kvbuf.at[j, s, :, pl.ds(0, 2 * HD)], sems.at[j, s])

    kvbuf[:, :, :, 2 * HD:] = jnp.ones(kvbuf.shape[:3] + (HD,), kvbuf.dtype)

    n_off = []
    for j in range(n_local):
        qb = qb0 + j
        block_copy(qb, dbuf.at[j], dsems.at[j]).start()

        def compact(s, n, j=j, qb=qb):
            b = bl_ref[j, s]
            off_ref[j, n] = b
            return n + (b != qb).astype(jnp.int32)

        n_j = lax.fori_loop(0, cnt_ref[j], compact, 0)
        n_off.append(n_j)
        n_pad = (n_j + group - 1) // group * group

        def pad(s, c, j=j, qb=qb):
            off_ref[j, s] = qb
            return c

        lax.fori_loop(n_j, n_pad, pad, 0)

        def issue(s, c, j=j):
            copy(j, s).start()
            return c

        lax.fori_loop(0, n_pad, issue, 0)

    rows = QH * BLK
    rowpos = lax.broadcasted_iota(jnp.int32, (rows, BLK), 0) % BLK
    col = lax.broadcasted_iota(jnp.int32, (rows, BLK), 1)
    causal = col <= rowpos
    dims = (((1,), (1,)), ((), ()))

    slot_of = lax.broadcasted_iota(jnp.int32, (rows, group * BLK), 1) // BLK

    def update(qs, kvb, carry, live=None):
        m, l, acc = carry
        k = kvb[:, :HD]
        v = kvb[:, HD:]
        sc = lax.dot_general(qs, k, dims, preferred_element_type=jnp.float32)
        if live is not None:
            sc = jnp.where(slot_of < live, sc, masked_score)
        m_new = jnp.maximum(m, jnp.max(sc, axis=1, keepdims=True) * scale)
        alpha = jnp.exp2(m - m_new)
        w = jnp.exp2(sc * scale - m_new)
        both = jnp.dot(w.astype(jnp.bfloat16), v, preferred_element_type=jnp.float32)
        l = alpha * l + both[:, HD:HD + 1]
        acc = alpha * acc + both[:, :HD]
        return m_new, l, acc

    for j in range(n_local):
        qb = qb0 + j
        qrows = q_ref[j * BLK:(j + 1) * BLK, :]
        qs = jnp.concatenate([qrows[:, h * HD:(h + 1) * HD] for h in range(QH)], axis=0)

        block_copy(qb, dbuf.at[j], dsems.at[j]).wait()
        kvd = dbuf[j]
        sc = lax.dot_general(qs, kvd[:, :HD], dims, preferred_element_type=jnp.float32) * scale
        m = jnp.max(jnp.where(causal, sc, masked_score), axis=1, keepdims=True)
        w = jnp.where(causal, jnp.exp2(sc - m), 0.0)
        l = jnp.sum(w, axis=1, keepdims=True)
        acc = jnp.dot(w.astype(jnp.bfloat16), kvd[:, HD:2 * HD], preferred_element_type=jnp.float32)

        def grouped(g, carry, j=j, qs=qs):
            first = g * group
            for i in range(group):
                copy(j, first + i).wait()
            kvb = kvbuf[j, pl.ds(first, group)].reshape(group * BLK, width)
            return update(qs, kvb, carry)

        def last(g, carry, j=j, qs=qs):
            first = g * group
            for i in range(group):
                copy(j, first + i).wait()
            kvb = kvbuf[j, pl.ds(first, group)].reshape(group * BLK, width)
            return update(qs, kvb, carry, live=n_off[j] - first)

        n_groups = n_off[j] // group
        carry = lax.fori_loop(0, n_groups, grouped, (m, l, acc))
        m, l, acc = lax.fori_loop(n_groups, (n_off[j] + group - 1) // group, last, carry)
        res = (acc / l).astype(out_ref.dtype)
        for h in range(QH):
            out_ref[j * BLK:(j + 1) * BLK, h * HD:(h + 1) * HD] = res[h * BLK:(h + 1) * BLK, :]


def shards(queries, key_cache, value_cache, block_list, block_count, *, n_pb, n_ka):
    kv_local = jnp.concatenate([key_cache, value_cache], axis=1)
    n_half = kv_local.shape[0] // BLK
    kv_pieces = []
    shard = None
    for h in range(n_half):
        part = kv_local[h * BLK:(h + 1) * BLK]
        if shard is not None:
            part, shard = lax.optimization_barrier((part, shard))
            kv_pieces += pieces_axis(shard, "ka", n_ka)
        shard = gather_axis(part, "pb", n_pb)
    kv_pieces += pieces_axis(shard, "ka", n_ka)

    p = lax.axis_index("pb")
    k = lax.axis_index("ka")
    rows_mine = queries.shape[0] // n_ka
    n_local = rows_mine // BLK
    listed = block_list.shape[1]
    q_mine = lax.dynamic_slice_in_dim(queries, k * rows_mine, rows_mine, 0)
    bl_mine = lax.dynamic_slice_in_dim(block_list, k * n_local, n_local, 0)
    cnt_mine = lax.dynamic_slice_in_dim(block_count, k * n_local, n_local, 0)
    qb0 = jnp.stack([(p * n_ka + k) * n_local, k]).astype(jnp.int32)

    kernel = functools.partial(
        attend_kernel, n_local=n_local, n_pieces=len(kv_pieces), n_ka=n_ka, group=32, scale=math.log2(math.e) / math.sqrt(HD)
    )
    return pl.pallas_call(
        kernel,
        out_shape=jax.ShapeDtypeStruct((rows_mine, queries.shape[1]), jnp.bfloat16),
        grid_spec=pltpu.PrefetchScalarGridSpec(
            num_scalar_prefetch=3,
            grid=(1,),
            in_specs=[
                pl.BlockSpec((rows_mine, queries.shape[1]), lambda i, *_: (0, 0)),
            ]
            + [pl.BlockSpec(memory_space=pl.ANY)] * len(kv_pieces),
            out_specs=pl.BlockSpec((rows_mine, queries.shape[1]), lambda i, *_: (0, 0)),
            scratch_shapes=[
                pltpu.SMEM((n_local, listed), jnp.int32),
                pltpu.VMEM((n_local, listed, BLK, kv_local.shape[1] + HD), jnp.bfloat16),
                pltpu.VMEM((n_local, BLK, kv_local.shape[1]), jnp.bfloat16),
                pltpu.SemaphoreType.DMA((n_local, listed)),
                pltpu.SemaphoreType.DMA((n_local,)),
            ],
        ),
        compiler_params=pltpu.CompilerParams(vmem_limit_bytes=48 * 1024 * 1024),
    )(bl_mine, cnt_mine, qb0, q_mine, *kv_pieces)


def solution(mesh):
    placed = (P("pb", None), P(("ka", "pb"), None), P(("ka", "pb"), None), P("pb", None), P("pb"))
    body = functools.partial(shards, n_pb=mesh.shape["pb"], n_ka=mesh.shape["ka"])
    return jax.shard_map(
        body, mesh=mesh, in_specs=placed, out_specs=P(("pb", "ka"), None), check_vma=False
    )
```

```python
import functools
import math

import jax
import jax.numpy as jnp
from jax import lax
from jax.experimental import pallas as pl
from jax.experimental.pallas import tpu as pltpu
from jax.sharding import PartitionSpec as P

HD = 128
QH = 4
BLK = 128

masked_score = -1e30


def gather_axis(local, axis, n):
    idx = lax.axis_index(axis)
    bits = n.bit_length() - 1
    held = local.reshape((1,) * bits + local.shape)
    for t in range(bits):
        b = n >> (t + 1)
        other = lax.ppermute(held, axis, [(i, i ^ b) for i in range(n)])
        upper = (idx // b) % 2 == 1
        held = jnp.where(
            upper,
            jnp.concatenate([other, held], axis=t),
            jnp.concatenate([held, other], axis=t),
        )
    return held.reshape((n * local.shape[0],) + local.shape[1:])


def pieces_axis(local, axis, n):
    idx_pieces = {0: local}
    b = n // 2
    while b >= 1:
        for x in sorted(idx_pieces):
            idx_pieces[x | b] = lax.ppermute(idx_pieces[x], axis, [(i, i ^ b) for i in range(n)])
        b //= 2
    return [idx_pieces[x] for x in range(n)]


def attend_kernel(bl_ref, cnt_ref, qb_ref, q_ref, *rest, n_local, n_pieces, n_ka, group, scale):
    kv_pieces = rest[:n_pieces]
    out_ref, off_ref, kvbuf, dbuf, sems, dsems = rest[n_pieces:]
    qb0 = qb_ref[0]
    me = qb_ref[1]
    row0 = me * n_local
    width = kvbuf.shape[-1]
    per_piece = kv_pieces[0].shape[0] // BLK
    n_half = n_pieces // n_ka

    class block_copy:
        def __init__(self, blk, dst, sem):
            self.blk, self.dst, self.sem = blk, dst, sem

        def start(self):
            per_shard = per_piece * n_half
            within = self.blk % per_shard
            which = (within % n_half) * n_ka + jnp.bitwise_xor(self.blk // per_shard, me)
            start = pl.multiple_of((within // n_half) * BLK, BLK)
            for x in range(n_pieces):
                @pl.when(which == x)
                def _(x=x, start=start):
                    pltpu.make_async_copy(kv_pieces[x].at[pl.ds(start, BLK), :], self.dst, self.sem).start()

        def wait(self):
            pltpu.make_async_copy(kv_pieces[0].at[pl.ds(0, BLK), :], self.dst, self.sem).wait()

    def copy(j, s):
        return block_copy(off_ref[j, s], kvbuf.at[j, s, :, pl.ds(0, 2 * HD)], sems.at[j, s])

    kvbuf[:, :, :, 2 * HD:] = jnp.ones(kvbuf.shape[:3] + (HD,), kvbuf.dtype)

    n_off = []
    for j in range(n_local):
        qb = qb0 + j
        block_copy(qb, dbuf.at[j], dsems.at[j]).start()

        def compact(s, n, j=j, qb=qb):
            b = bl_ref[row0 + j, s]
            off_ref[j, n] = b
            return n + (b != qb).astype(jnp.int32)

        n_j = lax.fori_loop(0, cnt_ref[row0 + j], compact, 0)
        n_off.append(n_j)
        n_pad = (n_j + group - 1) // group * group

        def pad(s, c, j=j, qb=qb):
            off_ref[j, s] = qb
            return c

        lax.fori_loop(n_j, n_pad, pad, 0)

        def issue(s, c, j=j):
            copy(j, s).start()
            return c

        lax.fori_loop(0, n_pad, issue, 0)

    rows = QH * BLK
    rowpos = lax.broadcasted_iota(jnp.int32, (rows, BLK), 0) % BLK
    col = lax.broadcasted_iota(jnp.int32, (rows, BLK), 1)
    causal = col <= rowpos
    dims = (((1,), (1,)), ((), ()))

    slot_of = lax.broadcasted_iota(jnp.int32, (rows, group * BLK), 1) // BLK

    def update(qs, kvb, carry, live=None):
        m, l, acc = carry
        k = kvb[:, :HD]
        v = kvb[:, HD:]
        sc = lax.dot_general(qs, k, dims, preferred_element_type=jnp.float32)
        if live is not None:
            sc = jnp.where(slot_of < live, sc, masked_score)
        m_new = jnp.maximum(m, jnp.max(sc, axis=1, keepdims=True) * scale)
        alpha = jnp.exp2(m - m_new)
        w = jnp.exp2(sc * scale - m_new)
        both = jnp.dot(w.astype(jnp.bfloat16), v, preferred_element_type=jnp.float32)
        l = alpha * l + both[:, HD:HD + 1]
        acc = alpha * acc + both[:, :HD]
        return m_new, l, acc

    for j in range(n_local):
        qb = qb0 + j
        qrows = q_ref[j * BLK:(j + 1) * BLK, :]
        qs = jnp.concatenate([qrows[:, h * HD:(h + 1) * HD] for h in range(QH)], axis=0)

        block_copy(qb, dbuf.at[j], dsems.at[j]).wait()
        kvd = dbuf[j]
        sc = lax.dot_general(qs, kvd[:, :HD], dims, preferred_element_type=jnp.float32) * scale
        m = jnp.max(jnp.where(causal, sc, masked_score), axis=1, keepdims=True)
        w = jnp.where(causal, jnp.exp2(sc - m), 0.0)
        l = jnp.sum(w, axis=1, keepdims=True)
        acc = jnp.dot(w.astype(jnp.bfloat16), kvd[:, HD:2 * HD], preferred_element_type=jnp.float32)

        def grouped(g, carry, j=j, qs=qs):
            first = g * group
            for i in range(group):
                copy(j, first + i).wait()
            kvb = kvbuf[j, pl.ds(first, group)].reshape(group * BLK, width)
            return update(qs, kvb, carry)

        def last(g, carry, j=j, qs=qs):
            first = g * group
            for i in range(group):
                copy(j, first + i).wait()
            kvb = kvbuf[j, pl.ds(first, group)].reshape(group * BLK, width)
            return update(qs, kvb, carry, live=n_off[j] - first)

        n_groups = n_off[j] // group
        carry = lax.fori_loop(0, n_groups, grouped, (m, l, acc))
        m, l, acc = lax.fori_loop(n_groups, (n_off[j] + group - 1) // group, last, carry)
        res = (acc / l).astype(out_ref.dtype)
        for h in range(QH):
            out_ref[j * BLK:(j + 1) * BLK, h * HD:(h + 1) * HD] = res[h * BLK:(h + 1) * BLK, :]


def shards(queries, key_cache, value_cache, block_list, block_count, *, n_pb, n_ka):
    kv_local = jnp.concatenate([key_cache, value_cache], axis=1)
    n_half = kv_local.shape[0] // BLK
    kv_pieces = []
    shard = None
    for h in range(n_half):
        part = kv_local[h * BLK:(h + 1) * BLK]
        if shard is not None:
            part, shard = lax.optimization_barrier((part, shard))
            kv_pieces += pieces_axis(shard, "ka", n_ka)
        shard = gather_axis(part, "pb", n_pb)
    kv_pieces += pieces_axis(shard, "ka", n_ka)

    p = lax.axis_index("pb")
    k = lax.axis_index("ka")
    rows_mine = queries.shape[0] // n_ka
    n_local = rows_mine // BLK
    listed = block_list.shape[1]
    qb0 = jnp.stack([(p * n_ka + k) * n_local, k]).astype(jnp.int32)

    kernel = functools.partial(
        attend_kernel, n_local=n_local, n_pieces=len(kv_pieces), n_ka=n_ka, group=16, scale=math.log2(math.e) / math.sqrt(HD)
    )
    return pl.pallas_call(
        kernel,
        out_shape=jax.ShapeDtypeStruct((rows_mine, queries.shape[1]), jnp.bfloat16),
        grid_spec=pltpu.PrefetchScalarGridSpec(
            num_scalar_prefetch=3,
            grid=(1,),
            in_specs=[
                pl.BlockSpec((rows_mine, queries.shape[1]), lambda i, bl, cnt, qb: (qb[1], 0)),
            ]
            + [pl.BlockSpec(memory_space=pl.ANY)] * len(kv_pieces),
            out_specs=pl.BlockSpec((rows_mine, queries.shape[1]), lambda i, *_: (0, 0)),
            scratch_shapes=[
                pltpu.SMEM((n_local, listed), jnp.int32),
                pltpu.VMEM((n_local, listed, BLK, kv_local.shape[1] + HD), jnp.bfloat16),
                pltpu.VMEM((n_local, BLK, kv_local.shape[1]), jnp.bfloat16),
                pltpu.SemaphoreType.DMA((n_local, listed)),
                pltpu.SemaphoreType.DMA((n_local,)),
            ],
        ),
        compiler_params=pltpu.CompilerParams(vmem_limit_bytes=48 * 1024 * 1024),
    )(block_list, block_count, qb0, queries, *kv_pieces)


def solution(mesh):
    placed = (P("pb", None), P(("ka", "pb"), None), P(("ka", "pb"), None), P("pb", None), P("pb"))
    body = functools.partial(shards, n_pb=mesh.shape["pb"], n_ka=mesh.shape["ka"])
    return jax.shard_map(
        body, mesh=mesh, in_specs=placed, out_specs=P(("pb", "ka"), None), check_vma=False
    )
```

```python
import functools
import math

import jax
import jax.numpy as jnp
from jax import lax
from jax.experimental import pallas as pl
from jax.experimental.pallas import tpu as pltpu
from jax.sharding import PartitionSpec as P

HD = 128
QH = 4
BLK = 128

masked_score = -1e30


def gather_axis(local, axis, n):
    idx = lax.axis_index(axis)
    bits = n.bit_length() - 1
    held = local.reshape((1,) * bits + local.shape)
    for t in range(bits):
        b = n >> (t + 1)
        other = lax.ppermute(held, axis, [(i, i ^ b) for i in range(n)])
        upper = (idx // b) % 2 == 1
        held = jnp.where(
            upper,
            jnp.concatenate([other, held], axis=t),
            jnp.concatenate([held, other], axis=t),
        )
    return held.reshape((n * local.shape[0],) + local.shape[1:])


def pieces_axis(local, axis, n):
    idx_pieces = {0: local}
    b = n // 2
    while b >= 1:
        for x in sorted(idx_pieces):
            idx_pieces[x | b] = lax.ppermute(idx_pieces[x], axis, [(i, i ^ b) for i in range(n)])
        b //= 2
    return [idx_pieces[x] for x in range(n)]


def attend_kernel(bl_ref, cnt_ref, qb_ref, q_ref, *rest, n_local, n_pieces, n_ka, group, scale, phase):
    n_refs = n_pieces - 1 if phase == 0 else 1
    kv_refs = rest[:n_refs]
    if phase == 0:
        m_io, l_io, acc_io, off_ref, kvbuf, dbuf, sems, dsems = rest[n_refs:]
    else:
        m_io, l_io, acc_io, out_ref, off_ref, kvbuf, dbuf, sems, dsems = rest[n_refs:]
    qb0 = qb_ref[0]
    me = qb_ref[1]
    row0 = me * n_local
    width = kvbuf.shape[-1]
    per_piece = kv_refs[0].shape[0] // BLK
    n_half = n_pieces // n_ka
    per_shard = per_piece * n_half
    final = n_pieces - 1

    def piece_of(blk):
        within = blk % per_shard
        return (within % n_half) * n_ka + jnp.bitwise_xor(blk // per_shard, me)

    def mine(blk):
        return piece_of(blk) != final if phase == 0 else piece_of(blk) == final

    class block_copy:
        def __init__(self, blk, dst, sem):
            self.blk, self.dst, self.sem = blk, dst, sem

        def start(self):
            start = pl.multiple_of(((self.blk % per_shard) // n_half) * BLK, BLK)
            if phase == 1:
                pltpu.make_async_copy(kv_refs[0].at[pl.ds(start, BLK), :], self.dst, self.sem).start()
                return
            which = piece_of(self.blk)
            for x in range(n_refs):
                @pl.when(which == x)
                def _(x=x, start=start):
                    pltpu.make_async_copy(kv_refs[x].at[pl.ds(start, BLK), :], self.dst, self.sem).start()

        def wait(self):
            pltpu.make_async_copy(kv_refs[0].at[pl.ds(0, BLK), :], self.dst, self.sem).wait()

    def copy(j, s):
        return block_copy(off_ref[j, s], kvbuf.at[j, s, :, pl.ds(0, 2 * HD)], sems.at[j, s])

    kvbuf[:, :, :, 2 * HD:] = jnp.ones(kvbuf.shape[:3] + (HD,), kvbuf.dtype)

    n_off = []
    diag_here = []
    for j in range(n_local):
        qb = qb0 + j
        here = mine(qb)
        diag_here.append(here)

        @pl.when(here)
        def _(j=j, qb=qb):
            block_copy(qb, dbuf.at[j], dsems.at[j]).start()

        def compact(s, n, j=j, qb=qb):
            b = bl_ref[row0 + j, s]
            off_ref[j, n] = b
            return n + jnp.logical_and(b != qb, mine(b)).astype(jnp.int32)

        n_j = lax.fori_loop(0, cnt_ref[row0 + j], compact, 0)
        n_off.append(n_j)
        n_pad = (n_j + group - 1) // group * group

        def pad(s, c, j=j, qb=qb):
            off_ref[j, s] = off_ref[j, 0]
            return c

        lax.fori_loop(n_j, n_pad, pad, 0)

        def issue(s, c, j=j):
            copy(j, s).start()
            return c

        lax.fori_loop(0, n_pad, issue, 0)

    rows = QH * BLK
    rowpos = lax.broadcasted_iota(jnp.int32, (rows, BLK), 0) % BLK
    col = lax.broadcasted_iota(jnp.int32, (rows, BLK), 1)
    causal = col <= rowpos
    dims = (((1,), (1,)), ((), ()))
    slot_of = lax.broadcasted_iota(jnp.int32, (rows, group * BLK), 1) // BLK

    def update(qs, kvb, carry, live=None):
        m, l, acc = carry
        k = kvb[:, :HD]
        v = kvb[:, HD:]
        sc = lax.dot_general(qs, k, dims, preferred_element_type=jnp.float32)
        if live is not None:
            sc = jnp.where(slot_of < live, sc, masked_score)
        m_new = jnp.maximum(m, jnp.max(sc, axis=1, keepdims=True) * scale)
        alpha = jnp.exp2(m - m_new)
        w = jnp.exp2(sc * scale - m_new)
        both = jnp.dot(w.astype(jnp.bfloat16), v, preferred_element_type=jnp.float32)
        l = alpha * l + both[:, HD:HD + 1]
        acc = alpha * acc + both[:, :HD]
        return m_new, l, acc

    for j in range(n_local):
        qb = qb0 + j
        qrows = q_ref[j * BLK:(j + 1) * BLK, :]
        qs = jnp.concatenate([qrows[:, h * HD:(h + 1) * HD] for h in range(QH)], axis=0)
        if phase == 0:
            carry = (
                jnp.full((rows, 1), masked_score, jnp.float32),
                jnp.zeros((rows, 1), jnp.float32),
                jnp.zeros((rows, HD), jnp.float32),
            )
        else:
            carry = (m_io[j], l_io[j], acc_io[j])

        def diag(carry, j=j, qb=qb, qs=qs):
            m, l, acc = carry
            block_copy(qb, dbuf.at[j], dsems.at[j]).wait()
            kvd = dbuf[j]
            sc = lax.dot_general(qs, kvd[:, :HD], dims, preferred_element_type=jnp.float32)
            m_new = jnp.maximum(m, jnp.max(jnp.where(causal, sc, masked_score), axis=1, keepdims=True) * scale)
            alpha = jnp.exp2(m - m_new)
            w = jnp.where(causal, jnp.exp2(sc * scale - m_new), 0.0)
            l = alpha * l + jnp.sum(w, axis=1, keepdims=True)
            acc = alpha * acc + jnp.dot(w.astype(jnp.bfloat16), kvd[:, HD:2 * HD], preferred_element_type=jnp.float32)
            return m_new, l, acc

        carry = lax.cond(diag_here[j], diag, lambda c: c, carry)

        def grouped(g, carry, j=j, qs=qs):
            first = g * group
            for i in range(group):
                copy(j, first + i).wait()
            kvb = kvbuf[j, pl.ds(first, group)].reshape(group * BLK, width)
            return update(qs, kvb, carry)

        def last(g, carry, j=j, qs=qs):
            first = g * group
            for i in range(group):
                copy(j, first + i).wait()
            kvb = kvbuf[j, pl.ds(first, group)].reshape(group * BLK, width)
            return update(qs, kvb, carry, live=n_off[j] - first)

        n_groups = n_off[j] // group
        carry = lax.fori_loop(0, n_groups, grouped, carry)
        m, l, acc = lax.fori_loop(n_groups, (n_off[j] + group - 1) // group, last, carry)
        if phase == 0:
            m_io[j] = m
            l_io[j] = l
            acc_io[j] = acc
        else:
            res = (acc / l).astype(out_ref.dtype)
            for h in range(QH):
                out_ref[j * BLK:(j + 1) * BLK, h * HD:(h + 1) * HD] = res[h * BLK:(h + 1) * BLK, :]


def shards(queries, key_cache, value_cache, block_list, block_count, *, n_pb, n_ka):
    kv_local = jnp.concatenate([key_cache, value_cache], axis=1)
    n_half = kv_local.shape[0] // BLK
    kv_pieces = []
    shard = None
    for h in range(n_half):
        part = kv_local[h * BLK:(h + 1) * BLK]
        if shard is not None:
            part, shard = lax.optimization_barrier((part, shard))
            kv_pieces += pieces_axis(shard, "ka", n_ka)
        shard = gather_axis(part, "pb", n_pb)
    kv_pieces += pieces_axis(shard, "ka", n_ka)

    p = lax.axis_index("pb")
    k = lax.axis_index("ka")
    rows_mine = queries.shape[0] // n_ka
    n_local = rows_mine // BLK
    listed = block_list.shape[1]
    qb0 = jnp.stack([(p * n_ka + k) * n_local, k]).astype(jnp.int32)

    rows = QH * BLK
    width = queries.shape[1]
    state_shapes = [
        jax.ShapeDtypeStruct((n_local, rows, 1), jnp.float32),
        jax.ShapeDtypeStruct((n_local, rows, 1), jnp.float32),
        jax.ShapeDtypeStruct((n_local, rows, HD), jnp.float32),
    ]
    state_specs = [pl.BlockSpec(st.shape, lambda i, *_: (0, 0, 0)) for st in state_shapes]
    q_spec = pl.BlockSpec((rows_mine, width), lambda i, bl, cnt, qb: (qb[1], 0))
    scratch = [
        pltpu.SMEM((n_local, listed), jnp.int32),
        pltpu.VMEM((n_local, listed, BLK, kv_local.shape[1] + HD), jnp.bfloat16),
        pltpu.VMEM((n_local, BLK, kv_local.shape[1]), jnp.bfloat16),
        pltpu.SemaphoreType.DMA((n_local, listed)),
        pltpu.SemaphoreType.DMA((n_local,)),
    ]
    params = pltpu.CompilerParams(vmem_limit_bytes=48 * 1024 * 1024)

    def phase_call(phase):
        return functools.partial(
            attend_kernel, n_local=n_local, n_pieces=len(kv_pieces), n_ka=n_ka,
            group=16, scale=math.log2(math.e) / math.sqrt(HD), phase=phase,
        )

    state = pl.pallas_call(
        phase_call(0),
        out_shape=state_shapes,
        grid_spec=pltpu.PrefetchScalarGridSpec(
            num_scalar_prefetch=3,
            grid=(1,),
            in_specs=[q_spec] + [pl.BlockSpec(memory_space=pl.ANY)] * (len(kv_pieces) - 1),
            out_specs=state_specs,
            scratch_shapes=scratch,
        ),
        compiler_params=params,
    )(block_list, block_count, qb0, queries, *kv_pieces[:-1])
    return pl.pallas_call(
        phase_call(1),
        out_shape=jax.ShapeDtypeStruct((rows_mine, width), jnp.bfloat16),
        grid_spec=pltpu.PrefetchScalarGridSpec(
            num_scalar_prefetch=3,
            grid=(1,),
            in_specs=[q_spec, pl.BlockSpec(memory_space=pl.ANY)] + state_specs,
            out_specs=pl.BlockSpec((rows_mine, width), lambda i, *_: (0, 0)),
            scratch_shapes=scratch,
        ),
        compiler_params=params,
    )(block_list, block_count, qb0, queries, kv_pieces[-1], *state)


def solution(mesh):
    placed = (P("pb", None), P(("ka", "pb"), None), P(("ka", "pb"), None), P("pb", None), P("pb"))
    body = functools.partial(shards, n_pb=mesh.shape["pb"], n_ka=mesh.shape["ka"])
    return jax.shard_map(
        body, mesh=mesh, in_specs=placed, out_specs=P(("pb", "ka"), None), check_vma=False
    )
```

```python
import functools
import math

import jax
import jax.numpy as jnp
from jax import lax
from jax.experimental import pallas as pl
from jax.experimental.pallas import tpu as pltpu
from jax.sharding import PartitionSpec as P

HD = 128
QH = 4
BLK = 128

masked_score = -1e30


def gather_axis(local, axis, n):
    idx = lax.axis_index(axis)
    bits = n.bit_length() - 1
    held = local.reshape((1,) * bits + local.shape)
    for t in range(bits):
        b = n >> (t + 1)
        other = lax.ppermute(held, axis, [(i, i ^ b) for i in range(n)])
        upper = (idx // b) % 2 == 1
        held = jnp.where(
            upper,
            jnp.concatenate([other, held], axis=t),
            jnp.concatenate([held, other], axis=t),
        )
    return held.reshape((n * local.shape[0],) + local.shape[1:])


def pieces_axis(local, axis, n):
    idx_pieces = {0: local}
    b = n // 2
    while b >= 1:
        for x in sorted(idx_pieces):
            idx_pieces[x | b] = lax.ppermute(idx_pieces[x], axis, [(i, i ^ b) for i in range(n)])
        b //= 2
    return [idx_pieces[x] for x in range(n)]


def attend_kernel(bl_ref, cnt_ref, qb_ref, q_ref, *rest, n_local, n_pieces, n_ka, group, scale):
    kv_pieces = rest[:n_pieces]
    out_ref, off_ref, kvbuf, dbuf, sems, dsems = rest[n_pieces:]
    qb0 = qb_ref[0]
    me = qb_ref[1]
    row0 = me * n_local
    width = kvbuf.shape[-1]
    per_piece = kv_pieces[0].shape[0] // BLK
    n_half = n_pieces // n_ka

    class block_copy:
        def __init__(self, blk, dst, sem):
            self.blk, self.dst, self.sem = blk, dst, sem

        def start(self):
            per_shard = per_piece * n_half
            within = self.blk % per_shard
            which = (within % n_half) * n_ka + jnp.bitwise_xor(self.blk // per_shard, me)
            start = pl.multiple_of((within // n_half) * BLK, BLK)
            for x in range(n_pieces):
                @pl.when(which == x)
                def _(x=x, start=start):
                    pltpu.make_async_copy(kv_pieces[x].at[pl.ds(start, BLK), :], self.dst, self.sem).start()

        def wait(self):
            pltpu.make_async_copy(kv_pieces[0].at[pl.ds(0, BLK), :], self.dst, self.sem).wait()

    def copy(j, s):
        return block_copy(off_ref[j, s], kvbuf.at[j, s, :, pl.ds(0, 2 * HD)], sems.at[j, s])

    kvbuf[:, :, :, 2 * HD:] = jnp.ones(kvbuf.shape[:3] + (HD,), kvbuf.dtype)

    n_off = []
    for j in range(n_local):
        qb = qb0 + j
        block_copy(qb, dbuf.at[j], dsems.at[j]).start()

        def compact(s, n, j=j, qb=qb):
            b = bl_ref[row0 + j, s]
            off_ref[j, n] = b
            return n + (b != qb).astype(jnp.int32)

        n_j = lax.fori_loop(0, cnt_ref[row0 + j], compact, 0)
        n_off.append(n_j)
        n_pad = (n_j + group - 1) // group * group

        def pad(s, c, j=j, qb=qb):
            off_ref[j, s] = qb
            return c

        lax.fori_loop(n_j, n_pad, pad, 0)

        def issue(s, c, j=j):
            copy(j, s).start()
            return c

        lax.fori_loop(0, n_pad, issue, 0)

    rows = QH * BLK
    rowpos = lax.broadcasted_iota(jnp.int32, (rows, BLK), 0) % BLK
    col = lax.broadcasted_iota(jnp.int32, (rows, BLK), 1)
    causal = col <= rowpos
    dims = (((1,), (1,)), ((), ()))

    slot_of = lax.broadcasted_iota(jnp.int32, (rows, group * BLK), 1) // BLK

    def update(qs, kvb, carry, live=None):
        m, l, acc = carry
        k = kvb[:, :HD]
        v = kvb[:, HD:]
        sc = lax.dot_general(qs, k, dims, preferred_element_type=jnp.float32)
        if live is not None:
            sc = jnp.where(slot_of < live, sc, masked_score)
        m_new = jnp.maximum(m, jnp.max(sc, axis=1, keepdims=True) * scale)
        alpha = jnp.exp2(m - m_new)
        w = jnp.exp2(sc * scale - m_new)
        both = jnp.dot(w.astype(jnp.bfloat16), v, preferred_element_type=jnp.float32)
        l = alpha * l + both[:, HD:HD + 1]
        acc = alpha * acc + both[:, :HD]
        return m_new, l, acc

    for j in range(n_local):
        qb = qb0 + j
        qrows = q_ref[j * BLK:(j + 1) * BLK, :]
        qs = jnp.concatenate([qrows[:, h * HD:(h + 1) * HD] for h in range(QH)], axis=0)

        block_copy(qb, dbuf.at[j], dsems.at[j]).wait()
        kvd = dbuf[j]
        sc = lax.dot_general(qs, kvd[:, :HD], dims, preferred_element_type=jnp.float32) * scale
        m = jnp.max(jnp.where(causal, sc, masked_score), axis=1, keepdims=True)
        w = jnp.where(causal, jnp.exp2(sc - m), 0.0)
        l = jnp.sum(w, axis=1, keepdims=True)
        acc = jnp.dot(w.astype(jnp.bfloat16), kvd[:, HD:2 * HD], preferred_element_type=jnp.float32)

        def grouped(g, carry, j=j, qs=qs):
            first = g * group
            for i in range(group):
                copy(j, first + i).wait()
            kvb = kvbuf[j, pl.ds(first, group)].reshape(group * BLK, width)
            return update(qs, kvb, carry)

        def last(g, carry, j=j, qs=qs):
            first = g * group
            for i in range(group):
                copy(j, first + i).wait()
            kvb = kvbuf[j, pl.ds(first, group)].reshape(group * BLK, width)
            return update(qs, kvb, carry, live=n_off[j] - first)

        n_groups = n_off[j] // group
        carry = lax.fori_loop(0, n_groups, grouped, (m, l, acc))
        m, l, acc = lax.fori_loop(n_groups, (n_off[j] + group - 1) // group, last, carry)
        res = (acc / l).astype(out_ref.dtype)
        for h in range(QH):
            out_ref[j * BLK:(j + 1) * BLK, h * HD:(h + 1) * HD] = res[h * BLK:(h + 1) * BLK, :]


def shards(queries, key_cache, value_cache, block_list, block_count, *, n_pb, n_ka):
    kv_local = jnp.concatenate([key_cache, value_cache], axis=1)
    n_half = kv_local.shape[0] // BLK
    kv_pieces = []
    for h in range(n_half):
        part = kv_local[h * BLK:(h + 1) * BLK]
        if h % 2 == 0:
            kv_pieces += pieces_axis(gather_axis(part, "pb", n_pb), "ka", n_ka)
            continue
        b = n_ka // 2
        across = lax.ppermute(part, "ka", [(i, i ^ b) for i in range(n_ka)])
        both = gather_axis(jnp.stack([part, across]), "pb", n_pb).reshape(n_pb, 2, BLK, part.shape[1])
        held = {0: both[:, 0].reshape(-1, part.shape[1]), b: both[:, 1].reshape(-1, part.shape[1])}
        step = b // 2
        while step >= 1:
            for x in sorted(held):
                held[x | step] = lax.ppermute(held[x], "ka", [(i, i ^ step) for i in range(n_ka)])
            step //= 2
        kv_pieces += [held[x] for x in range(n_ka)]

    p = lax.axis_index("pb")
    k = lax.axis_index("ka")
    rows_mine = queries.shape[0] // n_ka
    n_local = rows_mine // BLK
    listed = block_list.shape[1]
    qb0 = jnp.stack([(p * n_ka + k) * n_local, k]).astype(jnp.int32)

    kernel = functools.partial(
        attend_kernel, n_local=n_local, n_pieces=len(kv_pieces), n_ka=n_ka, group=16, scale=math.log2(math.e) / math.sqrt(HD)
    )
    return pl.pallas_call(
        kernel,
        out_shape=jax.ShapeDtypeStruct((rows_mine, queries.shape[1]), jnp.bfloat16),
        grid_spec=pltpu.PrefetchScalarGridSpec(
            num_scalar_prefetch=3,
            grid=(1,),
            in_specs=[
                pl.BlockSpec((rows_mine, queries.shape[1]), lambda i, bl, cnt, qb: (qb[1], 0)),
            ]
            + [pl.BlockSpec(memory_space=pl.ANY)] * len(kv_pieces),
            out_specs=pl.BlockSpec((rows_mine, queries.shape[1]), lambda i, *_: (0, 0)),
            scratch_shapes=[
                pltpu.SMEM((n_local, listed), jnp.int32),
                pltpu.VMEM((n_local, listed, BLK, kv_local.shape[1] + HD), jnp.bfloat16),
                pltpu.VMEM((n_local, BLK, kv_local.shape[1]), jnp.bfloat16),
                pltpu.SemaphoreType.DMA((n_local, listed)),
                pltpu.SemaphoreType.DMA((n_local,)),
            ],
        ),
        compiler_params=pltpu.CompilerParams(vmem_limit_bytes=48 * 1024 * 1024),
    )(block_list, block_count, qb0, queries, *kv_pieces)


def solution(mesh):
    placed = (P("pb", None), P(("ka", "pb"), None), P(("ka", "pb"), None), P("pb", None), P("pb"))
    body = functools.partial(shards, n_pb=mesh.shape["pb"], n_ka=mesh.shape["ka"])
    return jax.shard_map(
        body, mesh=mesh, in_specs=placed, out_specs=P(("pb", "ka"), None), check_vma=False
    )
```

```python
import functools
import math

import jax
import jax.numpy as jnp
from jax import lax
from jax.experimental import pallas as pl
from jax.experimental.pallas import tpu as pltpu
from jax.sharding import PartitionSpec as P

HD = 128
QH = 4
BLK = 128

masked_score = -1e30


def gather_axis(local, axis, n):
    idx = lax.axis_index(axis)
    bits = n.bit_length() - 1
    held = local.reshape((1,) * bits + local.shape)
    for t in range(bits):
        b = n >> (t + 1)
        other = lax.ppermute(held, axis, [(i, i ^ b) for i in range(n)])
        upper = (idx // b) % 2 == 1
        held = jnp.where(
            upper,
            jnp.concatenate([other, held], axis=t),
            jnp.concatenate([held, other], axis=t),
        )
    return held.reshape((n * local.shape[0],) + local.shape[1:])


def pieces_axis(local, axis, n):
    idx_pieces = {0: local}
    b = n // 2
    while b >= 1:
        for x in sorted(idx_pieces):
            idx_pieces[x | b] = lax.ppermute(idx_pieces[x], axis, [(i, i ^ b) for i in range(n)])
        b //= 2
    return [idx_pieces[x] for x in range(n)]


def attend_kernel(bl_ref, cnt_ref, qb_ref, q_ref, *rest, n_local, n_pieces, n_ka, group, scale):
    kv_pieces = rest[:n_pieces]
    out_ref, off_ref, kvbuf, dbuf, sems, dsems = rest[n_pieces:]
    qb0 = qb_ref[0]
    me = qb_ref[1]
    row0 = me * n_local
    width = kvbuf.shape[-1]
    per_piece = kv_pieces[0].shape[0] // BLK
    n_half = n_pieces // n_ka

    class block_copy:
        def __init__(self, blk, dst, sem):
            self.blk, self.dst, self.sem = blk, dst, sem

        def start(self):
            per_shard = per_piece * n_half
            within = self.blk % per_shard
            which = (within % n_half) * n_ka + jnp.bitwise_xor(self.blk // per_shard, me)
            start = pl.multiple_of((within // n_half) * BLK, BLK)
            for x in range(n_pieces):
                @pl.when(which == x)
                def _(x=x, start=start):
                    pltpu.make_async_copy(kv_pieces[x].at[pl.ds(start, BLK), :], self.dst, self.sem).start()

        def wait(self):
            pltpu.make_async_copy(kv_pieces[0].at[pl.ds(0, BLK), :], self.dst, self.sem).wait()

    def copy(j, s):
        return block_copy(off_ref[j, s], kvbuf.at[j, s, :, pl.ds(0, 2 * HD)], sems.at[j, s])

    kvbuf[:, :, :, 2 * HD:] = jnp.ones(kvbuf.shape[:3] + (HD,), kvbuf.dtype)

    n_off = []
    for j in range(n_local):
        qb = qb0 + j
        block_copy(qb, dbuf.at[j], dsems.at[j]).start()

        def compact(s, n, j=j, qb=qb):
            b = bl_ref[row0 + j, s]
            off_ref[j, n] = b
            return n + (b != qb).astype(jnp.int32)

        n_j = lax.fori_loop(0, cnt_ref[row0 + j], compact, 0)
        n_off.append(n_j)
        n_pad = (n_j + group - 1) // group * group

        def pad(s, c, j=j, qb=qb):
            off_ref[j, s] = qb
            return c

        lax.fori_loop(n_j, n_pad, pad, 0)

        def issue(s, c, j=j):
            copy(j, s).start()
            return c

        lax.fori_loop(0, n_pad, issue, 0)

    rows = QH * BLK
    rowpos = lax.broadcasted_iota(jnp.int32, (rows, BLK), 0) % BLK
    col = lax.broadcasted_iota(jnp.int32, (rows, BLK), 1)
    causal = col <= rowpos
    dims = (((1,), (1,)), ((), ()))

    slot_of = lax.broadcasted_iota(jnp.int32, (rows, group * BLK), 1) // BLK

    def update(qs, kvb, carry, live=None):
        m, l, acc = carry
        k = kvb[:, :HD]
        v = kvb[:, HD:]
        sc = lax.dot_general(qs, k, dims, preferred_element_type=jnp.float32)
        if live is not None:
            sc = jnp.where(slot_of < live, sc, masked_score)
        m_new = jnp.maximum(m, jnp.max(sc, axis=1, keepdims=True) * scale)
        alpha = jnp.exp2(m - m_new)
        w = jnp.exp2(sc * scale - m_new)
        both = jnp.dot(w.astype(jnp.bfloat16), v, preferred_element_type=jnp.float32)
        l = alpha * l + both[:, HD:HD + 1]
        acc = alpha * acc + both[:, :HD]
        return m_new, l, acc

    for j in range(n_local):
        qb = qb0 + j
        qrows = q_ref[j * BLK:(j + 1) * BLK, :]
        qs = jnp.concatenate([qrows[:, h * HD:(h + 1) * HD] for h in range(QH)], axis=0)

        block_copy(qb, dbuf.at[j], dsems.at[j]).wait()
        kvd = dbuf[j]
        sc = lax.dot_general(qs, kvd[:, :HD], dims, preferred_element_type=jnp.float32) * scale
        m = jnp.max(jnp.where(causal, sc, masked_score), axis=1, keepdims=True)
        w = jnp.where(causal, jnp.exp2(sc - m), 0.0)
        l = jnp.sum(w, axis=1, keepdims=True)
        acc = jnp.dot(w.astype(jnp.bfloat16), kvd[:, HD:2 * HD], preferred_element_type=jnp.float32)

        def grouped(g, carry, j=j, qs=qs):
            first = g * group
            for i in range(group):
                copy(j, first + i).wait()
            kvb = kvbuf[j, pl.ds(first, group)].reshape(group * BLK, width)
            return update(qs, kvb, carry)

        def last(g, carry, j=j, qs=qs):
            first = g * group
            for i in range(group):
                copy(j, first + i).wait()
            kvb = kvbuf[j, pl.ds(first, group)].reshape(group * BLK, width)
            return update(qs, kvb, carry, live=n_off[j] - first)

        n_groups = n_off[j] // group
        carry = lax.fori_loop(0, n_groups, grouped, (m, l, acc))
        m, l, acc = lax.fori_loop(n_groups, (n_off[j] + group - 1) // group, last, carry)
        res = (acc / l).astype(out_ref.dtype)
        for h in range(QH):
            out_ref[j * BLK:(j + 1) * BLK, h * HD:(h + 1) * HD] = res[h * BLK:(h + 1) * BLK, :]


def shards(queries, key_cache, value_cache, block_list, block_count, *, n_pb, n_ka):
    kv_local = jnp.concatenate([key_cache, value_cache], axis=1)
    n_half = kv_local.shape[0] // BLK
    kv_pieces = []
    shard = None
    for h in range(n_half):
        part = kv_local[h * BLK:(h + 1) * BLK]
        if h % 2 == 0:
            shard = gather_axis(part, "pb", n_pb)
            continue
        b = n_ka // 2
        across = lax.ppermute(part, "ka", [(i, i ^ b) for i in range(n_ka)])
        pair, shard = lax.optimization_barrier((jnp.stack([part, across]), shard))
        kv_pieces += pieces_axis(shard, "ka", n_ka)
        shard = None
        both = gather_axis(pair, "pb", n_pb).reshape(n_pb, 2, BLK, part.shape[1])
        held = {0: both[:, 0].reshape(-1, part.shape[1]), b: both[:, 1].reshape(-1, part.shape[1])}
        step = b // 2
        while step >= 1:
            for x in sorted(held):
                held[x | step] = lax.ppermute(held[x], "ka", [(i, i ^ step) for i in range(n_ka)])
            step //= 2
        kv_pieces += [held[x] for x in range(n_ka)]
    if shard is not None:
        kv_pieces += pieces_axis(shard, "ka", n_ka)

    p = lax.axis_index("pb")
    k = lax.axis_index("ka")
    rows_mine = queries.shape[0] // n_ka
    n_local = rows_mine // BLK
    listed = block_list.shape[1]
    qb0 = jnp.stack([(p * n_ka + k) * n_local, k]).astype(jnp.int32)

    kernel = functools.partial(
        attend_kernel, n_local=n_local, n_pieces=len(kv_pieces), n_ka=n_ka, group=16, scale=math.log2(math.e) / math.sqrt(HD)
    )
    return pl.pallas_call(
        kernel,
        out_shape=jax.ShapeDtypeStruct((rows_mine, queries.shape[1]), jnp.bfloat16),
        grid_spec=pltpu.PrefetchScalarGridSpec(
            num_scalar_prefetch=3,
            grid=(1,),
            in_specs=[
                pl.BlockSpec((rows_mine, queries.shape[1]), lambda i, bl, cnt, qb: (qb[1], 0)),
            ]
            + [pl.BlockSpec(memory_space=pl.ANY)] * len(kv_pieces),
            out_specs=pl.BlockSpec((rows_mine, queries.shape[1]), lambda i, *_: (0, 0)),
            scratch_shapes=[
                pltpu.SMEM((n_local, listed), jnp.int32),
                pltpu.VMEM((n_local, listed, BLK, kv_local.shape[1] + HD), jnp.bfloat16),
                pltpu.VMEM((n_local, BLK, kv_local.shape[1]), jnp.bfloat16),
                pltpu.SemaphoreType.DMA((n_local, listed)),
                pltpu.SemaphoreType.DMA((n_local,)),
            ],
        ),
        compiler_params=pltpu.CompilerParams(vmem_limit_bytes=48 * 1024 * 1024),
    )(block_list, block_count, qb0, queries, *kv_pieces)


def solution(mesh):
    placed = (P("pb", None), P(("ka", "pb"), None), P(("ka", "pb"), None), P("pb", None), P("pb"))
    body = functools.partial(shards, n_pb=mesh.shape["pb"], n_ka=mesh.shape["ka"])
    return jax.shard_map(
        body, mesh=mesh, in_specs=placed, out_specs=P(("pb", "ka"), None), check_vma=False
    )
```

```python
import functools
import math

import jax
import jax.numpy as jnp
from jax import lax
from jax.experimental import pallas as pl
from jax.experimental.pallas import tpu as pltpu
from jax.sharding import PartitionSpec as P

HD = 128
QH = 4
BLK = 128

masked_score = -1e30


def gather_axis(local, axis, n):
    idx = lax.axis_index(axis)
    bits = n.bit_length() - 1
    held = local.reshape((1,) * bits + local.shape)
    for t in range(bits):
        b = n >> (t + 1)
        other = lax.ppermute(held, axis, [(i, i ^ b) for i in range(n)])
        upper = (idx // b) % 2 == 1
        held = jnp.where(
            upper,
            jnp.concatenate([other, held], axis=t),
            jnp.concatenate([held, other], axis=t),
        )
    return held.reshape((n * local.shape[0],) + local.shape[1:])


def pieces_axis(local, axis, n):
    idx_pieces = {0: local}
    b = n // 2
    while b >= 1:
        for x in sorted(idx_pieces):
            idx_pieces[x | b] = lax.ppermute(idx_pieces[x], axis, [(i, i ^ b) for i in range(n)])
        b //= 2
    return [idx_pieces[x] for x in range(n)]


def attend_kernel(bl_ref, cnt_ref, qb_ref, q_ref, *rest, n_local, sources, n_ka, group, scale):
    n_pieces = len(sources)
    n_direct = sum(1 for kind, _ in sources if kind == 0)
    direct = rest[:n_direct]
    fwd = rest[n_direct]
    out_ref, off_ref, kvbuf, dbuf, sems, dsems = rest[n_direct + 1:]
    kv_pieces = [direct[i] if kind == 0 else fwd.at[i] for kind, i in sources]
    qb0 = qb_ref[0]
    me = qb_ref[1]
    row0 = me * n_local
    width = kvbuf.shape[-1]
    per_piece = kv_pieces[0].shape[0] // BLK
    n_half = n_pieces // n_ka

    class block_copy:
        def __init__(self, blk, dst, sem):
            self.blk, self.dst, self.sem = blk, dst, sem

        def start(self):
            per_shard = per_piece * n_half
            within = self.blk % per_shard
            which = (within % n_half) * n_ka + jnp.bitwise_xor(self.blk // per_shard, me)
            start = pl.multiple_of((within // n_half) * BLK, BLK)
            for x in range(n_pieces):
                @pl.when(which == x)
                def _(x=x, start=start):
                    pltpu.make_async_copy(kv_pieces[x].at[pl.ds(start, BLK), :], self.dst, self.sem).start()

        def wait(self):
            pltpu.make_async_copy(kv_pieces[0].at[pl.ds(0, BLK), :], self.dst, self.sem).wait()

    def copy(j, s):
        return block_copy(off_ref[j, s], kvbuf.at[j, s, :, pl.ds(0, 2 * HD)], sems.at[j, s])

    kvbuf[:, :, :, 2 * HD:] = jnp.ones(kvbuf.shape[:3] + (HD,), kvbuf.dtype)

    n_off = []
    for j in range(n_local):
        qb = qb0 + j
        block_copy(qb, dbuf.at[j], dsems.at[j]).start()

        def compact(s, n, j=j, qb=qb):
            b = bl_ref[row0 + j, s]
            off_ref[j, n] = b
            return n + (b != qb).astype(jnp.int32)

        n_j = lax.fori_loop(0, cnt_ref[row0 + j], compact, 0)
        n_off.append(n_j)
        n_pad = (n_j + group - 1) // group * group

        def pad(s, c, j=j, qb=qb):
            off_ref[j, s] = qb
            return c

        lax.fori_loop(n_j, n_pad, pad, 0)

        def issue(s, c, j=j):
            copy(j, s).start()
            return c

        lax.fori_loop(0, n_pad, issue, 0)

    rows = QH * BLK
    rowpos = lax.broadcasted_iota(jnp.int32, (rows, BLK), 0) % BLK
    col = lax.broadcasted_iota(jnp.int32, (rows, BLK), 1)
    causal = col <= rowpos
    dims = (((1,), (1,)), ((), ()))

    slot_of = lax.broadcasted_iota(jnp.int32, (rows, group * BLK), 1) // BLK

    def update(qs, kvb, carry, live=None):
        m, l, acc = carry
        k = kvb[:, :HD]
        v = kvb[:, HD:]
        sc = lax.dot_general(qs, k, dims, preferred_element_type=jnp.float32)
        if live is not None:
            sc = jnp.where(slot_of < live, sc, masked_score)
        m_new = jnp.maximum(m, jnp.max(sc, axis=1, keepdims=True) * scale)
        alpha = jnp.exp2(m - m_new)
        w = jnp.exp2(sc * scale - m_new)
        both = jnp.dot(w.astype(jnp.bfloat16), v, preferred_element_type=jnp.float32)
        l = alpha * l + both[:, HD:HD + 1]
        acc = alpha * acc + both[:, :HD]
        return m_new, l, acc

    for j in range(n_local):
        qb = qb0 + j
        qrows = q_ref[j * BLK:(j + 1) * BLK, :]
        qs = jnp.concatenate([qrows[:, h * HD:(h + 1) * HD] for h in range(QH)], axis=0)

        block_copy(qb, dbuf.at[j], dsems.at[j]).wait()
        kvd = dbuf[j]
        sc = lax.dot_general(qs, kvd[:, :HD], dims, preferred_element_type=jnp.float32) * scale
        m = jnp.max(jnp.where(causal, sc, masked_score), axis=1, keepdims=True)
        w = jnp.where(causal, jnp.exp2(sc - m), 0.0)
        l = jnp.sum(w, axis=1, keepdims=True)
        acc = jnp.dot(w.astype(jnp.bfloat16), kvd[:, HD:2 * HD], preferred_element_type=jnp.float32)

        def grouped(g, carry, j=j, qs=qs):
            first = g * group
            for i in range(group):
                copy(j, first + i).wait()
            kvb = kvbuf[j, pl.ds(first, group)].reshape(group * BLK, width)
            return update(qs, kvb, carry)

        def last(g, carry, j=j, qs=qs):
            first = g * group
            for i in range(group):
                copy(j, first + i).wait()
            kvb = kvbuf[j, pl.ds(first, group)].reshape(group * BLK, width)
            return update(qs, kvb, carry, live=n_off[j] - first)

        n_groups = n_off[j] // group
        carry = lax.fori_loop(0, n_groups, grouped, (m, l, acc))
        m, l, acc = lax.fori_loop(n_groups, (n_off[j] + group - 1) // group, last, carry)
        res = (acc / l).astype(out_ref.dtype)
        for h in range(QH):
            out_ref[j * BLK:(j + 1) * BLK, h * HD:(h + 1) * HD] = res[h * BLK:(h + 1) * BLK, :]


def shards(queries, key_cache, value_cache, block_list, block_count, *, n_pb, n_ka):
    kv_local = jnp.concatenate([key_cache, value_cache], axis=1)
    n_half = kv_local.shape[0] // BLK
    halves = []
    shard = None
    b = n_ka // 2
    for h in range(n_half):
        part = kv_local[h * BLK:(h + 1) * BLK]
        if h % 2 == 0:
            shard = gather_axis(part, "pb", n_pb)
            continue
        across = lax.ppermute(part, "ka", [(i, i ^ b) for i in range(n_ka)])
        pair, shard = lax.optimization_barrier((jnp.stack([part, across]), shard))
        halves.append({0: shard})
        shard = None
        both = gather_axis(pair, "pb", n_pb).reshape(n_pb, 2, BLK, part.shape[1])
        halves.append({0: both[:, 0].reshape(-1, part.shape[1]), b: both[:, 1].reshape(-1, part.shape[1])})
    if shard is not None:
        halves.append({0: shard})
    for held in halves:
        step = b
        while step >= 2:
            for x in sorted(held):
                if x & step == 0 and (x | step) not in held:
                    held[x | step] = lax.ppermute(held[x], "ka", [(i, i ^ step) for i in range(n_ka)])
            step //= 2
    order = [(h, x) for h in range(len(halves)) for x in sorted(halves[h])]
    fwd = lax.ppermute(jnp.stack([halves[h][x] for h, x in order]), "ka", [(i, i ^ 1) for i in range(n_ka)])
    direct = [halves[h][x] for h, x in order]
    sources = []
    for h in range(len(halves)):
        for x in range(n_ka):
            if x % 2 == 0:
                sources.append((0, order.index((h, x))))
            else:
                sources.append((1, order.index((h, x - 1))))
    kv_pieces = direct + [fwd]

    p = lax.axis_index("pb")
    k = lax.axis_index("ka")
    rows_mine = queries.shape[0] // n_ka
    n_local = rows_mine // BLK
    listed = block_list.shape[1]
    qb0 = jnp.stack([(p * n_ka + k) * n_local, k]).astype(jnp.int32)

    kernel = functools.partial(
        attend_kernel, n_local=n_local, sources=tuple(sources), n_ka=n_ka, group=16, scale=math.log2(math.e) / math.sqrt(HD)
    )
    return pl.pallas_call(
        kernel,
        out_shape=jax.ShapeDtypeStruct((rows_mine, queries.shape[1]), jnp.bfloat16),
        grid_spec=pltpu.PrefetchScalarGridSpec(
            num_scalar_prefetch=3,
            grid=(1,),
            in_specs=[
                pl.BlockSpec((rows_mine, queries.shape[1]), lambda i, bl, cnt, qb: (qb[1], 0)),
            ]
            + [pl.BlockSpec(memory_space=pl.ANY)] * len(kv_pieces),
            out_specs=pl.BlockSpec((rows_mine, queries.shape[1]), lambda i, *_: (0, 0)),
            scratch_shapes=[
                pltpu.SMEM((n_local, listed), jnp.int32),
                pltpu.VMEM((n_local, listed, BLK, kv_local.shape[1] + HD), jnp.bfloat16),
                pltpu.VMEM((n_local, BLK, kv_local.shape[1]), jnp.bfloat16),
                pltpu.SemaphoreType.DMA((n_local, listed)),
                pltpu.SemaphoreType.DMA((n_local,)),
            ],
        ),
        compiler_params=pltpu.CompilerParams(vmem_limit_bytes=48 * 1024 * 1024),
    )(block_list, block_count, qb0, queries, *kv_pieces)


def solution(mesh):
    placed = (P("pb", None), P(("ka", "pb"), None), P(("ka", "pb"), None), P("pb", None), P("pb"))
    body = functools.partial(shards, n_pb=mesh.shape["pb"], n_ka=mesh.shape["ka"])
    return jax.shard_map(
        body, mesh=mesh, in_specs=placed, out_specs=P(("pb", "ka"), None), check_vma=False
    )
```

```python
import functools
import math

import jax
import jax.numpy as jnp
from jax import lax
from jax.experimental import pallas as pl
from jax.experimental.pallas import tpu as pltpu
from jax.sharding import PartitionSpec as P

HD = 128
QH = 4
BLK = 128

masked_score = -1e30


def gather_axis(local, axis, n):
    idx = lax.axis_index(axis)
    bits = n.bit_length() - 1
    held = local.reshape((1,) * bits + local.shape)
    for t in range(bits):
        b = n >> (t + 1)
        other = lax.ppermute(held, axis, [(i, i ^ b) for i in range(n)])
        upper = (idx // b) % 2 == 1
        held = jnp.where(
            upper,
            jnp.concatenate([other, held], axis=t),
            jnp.concatenate([held, other], axis=t),
        )
    return held.reshape((n * local.shape[0],) + local.shape[1:])


def pieces_axis(local, axis, n):
    idx_pieces = {0: local}
    b = n // 2
    while b >= 1:
        for x in sorted(idx_pieces):
            idx_pieces[x | b] = lax.ppermute(idx_pieces[x], axis, [(i, i ^ b) for i in range(n)])
        b //= 2
    return [idx_pieces[x] for x in range(n)]


def attend_kernel(bl_ref, cnt_ref, qb_ref, q_ref, *rest, n_local, sources, n_refs, n_ka, group, scale):
    n_pieces = len(sources)
    kv_pieces = rest[:n_refs]
    out_ref, off_ref, kvbuf, dbuf, sems, dsems = rest[n_refs:]
    qb0 = qb_ref[0]
    me = qb_ref[1]
    row0 = me * n_local
    width = kvbuf.shape[-1]
    per_piece = kv_pieces[0].shape[0] // BLK
    assert sources[0] == (0, -1)
    n_half = n_pieces // n_ka

    class block_copy:
        def __init__(self, blk, dst, sem):
            self.blk, self.dst, self.sem = blk, dst, sem

        def start(self):
            per_shard = per_piece * n_half
            within = self.blk % per_shard
            which = (within % n_half) * n_ka + jnp.bitwise_xor(self.blk // per_shard, me)
            start = pl.multiple_of((within // n_half) * BLK, BLK)
            chunk = within // n_half
            for x in range(n_pieces):
                @pl.when(which == x)
                def _(x=x, start=start, chunk=chunk):
                    ref_i, pair = sources[x]
                    if pair < 0:
                        src = kv_pieces[ref_i].at[pl.ds(start, BLK), :]
                    else:
                        src = kv_pieces[ref_i].at[chunk, pair]
                    pltpu.make_async_copy(src, self.dst, self.sem).start()

        def wait(self):
            pltpu.make_async_copy(kv_pieces[0].at[pl.ds(0, BLK), :], self.dst, self.sem).wait()

    def copy(j, s):
        return block_copy(off_ref[j, s], kvbuf.at[j, s, :, pl.ds(0, 2 * HD)], sems.at[j, s])

    kvbuf[:, :, :, 2 * HD:] = jnp.ones(kvbuf.shape[:3] + (HD,), kvbuf.dtype)

    n_off = []
    for j in range(n_local):
        qb = qb0 + j
        block_copy(qb, dbuf.at[j], dsems.at[j]).start()

        def compact(s, n, j=j, qb=qb):
            b = bl_ref[row0 + j, s]
            off_ref[j, n] = b
            return n + (b != qb).astype(jnp.int32)

        n_j = lax.fori_loop(0, cnt_ref[row0 + j], compact, 0)
        n_off.append(n_j)
        n_pad = (n_j + group - 1) // group * group

        def pad(s, c, j=j, qb=qb):
            off_ref[j, s] = qb
            return c

        lax.fori_loop(n_j, n_pad, pad, 0)

        def issue(s, c, j=j):
            copy(j, s).start()
            return c

        lax.fori_loop(0, n_pad, issue, 0)

    rows = QH * BLK
    rowpos = lax.broadcasted_iota(jnp.int32, (rows, BLK), 0) % BLK
    col = lax.broadcasted_iota(jnp.int32, (rows, BLK), 1)
    causal = col <= rowpos
    dims = (((1,), (1,)), ((), ()))

    slot_of = lax.broadcasted_iota(jnp.int32, (rows, group * BLK), 1) // BLK

    def update(qs, kvb, carry, live=None):
        m, l, acc = carry
        k = kvb[:, :HD]
        v = kvb[:, HD:]
        sc = lax.dot_general(qs, k, dims, preferred_element_type=jnp.float32)
        if live is not None:
            sc = jnp.where(slot_of < live, sc, masked_score)
        m_new = jnp.maximum(m, jnp.max(sc, axis=1, keepdims=True) * scale)
        alpha = jnp.exp2(m - m_new)
        w = jnp.exp2(sc * scale - m_new)
        both = jnp.dot(w.astype(jnp.bfloat16), v, preferred_element_type=jnp.float32)
        l = alpha * l + both[:, HD:HD + 1]
        acc = alpha * acc + both[:, :HD]
        return m_new, l, acc

    for j in range(n_local):
        qb = qb0 + j
        qrows = q_ref[j * BLK:(j + 1) * BLK, :]
        qs = jnp.concatenate([qrows[:, h * HD:(h + 1) * HD] for h in range(QH)], axis=0)

        block_copy(qb, dbuf.at[j], dsems.at[j]).wait()
        kvd = dbuf[j]
        sc = lax.dot_general(qs, kvd[:, :HD], dims, preferred_element_type=jnp.float32) * scale
        m = jnp.max(jnp.where(causal, sc, masked_score), axis=1, keepdims=True)
        w = jnp.where(causal, jnp.exp2(sc - m), 0.0)
        l = jnp.sum(w, axis=1, keepdims=True)
        acc = jnp.dot(w.astype(jnp.bfloat16), kvd[:, HD:2 * HD], preferred_element_type=jnp.float32)

        def grouped(g, carry, j=j, qs=qs):
            first = g * group
            for i in range(group):
                copy(j, first + i).wait()
            kvb = kvbuf[j, pl.ds(first, group)].reshape(group * BLK, width)
            return update(qs, kvb, carry)

        def last(g, carry, j=j, qs=qs):
            first = g * group
            for i in range(group):
                copy(j, first + i).wait()
            kvb = kvbuf[j, pl.ds(first, group)].reshape(group * BLK, width)
            return update(qs, kvb, carry, live=n_off[j] - first)

        n_groups = n_off[j] // group
        carry = lax.fori_loop(0, n_groups, grouped, (m, l, acc))
        m, l, acc = lax.fori_loop(n_groups, (n_off[j] + group - 1) // group, last, carry)
        res = (acc / l).astype(out_ref.dtype)
        for h in range(QH):
            out_ref[j * BLK:(j + 1) * BLK, h * HD:(h + 1) * HD] = res[h * BLK:(h + 1) * BLK, :]


def shards(queries, key_cache, value_cache, block_list, block_count, *, n_pb, n_ka):
    kv_local = jnp.concatenate([key_cache, value_cache], axis=1)
    n_half = kv_local.shape[0] // BLK
    assert n_half == 2 and n_ka == 4
    part0, part1 = kv_local[:BLK], kv_local[BLK:]
    shard = gather_axis(part0, "pb", n_pb)
    across = lax.ppermute(part1, "ka", [(i, i ^ 2) for i in range(n_ka)])
    pair, shard = lax.optimization_barrier((jnp.stack([part1, across]), shard))
    kv_pieces = pieces_axis(shard, "ka", n_ka)
    both = gather_axis(pair, "pb", n_pb).reshape(n_pb, 2, BLK, part1.shape[1])
    kv_pieces += [both, lax.ppermute(both, "ka", [(i, i ^ 1) for i in range(n_ka)])]
    sources = [(x, -1) for x in range(n_ka)] + [(4, 0), (5, 0), (4, 1), (5, 1)]

    p = lax.axis_index("pb")
    k = lax.axis_index("ka")
    rows_mine = queries.shape[0] // n_ka
    n_local = rows_mine // BLK
    listed = block_list.shape[1]
    qb0 = jnp.stack([(p * n_ka + k) * n_local, k]).astype(jnp.int32)

    kernel = functools.partial(
        attend_kernel, n_local=n_local, sources=tuple(sources), n_refs=len(kv_pieces), n_ka=n_ka, group=16, scale=math.log2(math.e) / math.sqrt(HD)
    )
    return pl.pallas_call(
        kernel,
        out_shape=jax.ShapeDtypeStruct((rows_mine, queries.shape[1]), jnp.bfloat16),
        grid_spec=pltpu.PrefetchScalarGridSpec(
            num_scalar_prefetch=3,
            grid=(1,),
            in_specs=[
                pl.BlockSpec((rows_mine, queries.shape[1]), lambda i, bl, cnt, qb: (qb[1], 0)),
            ]
            + [pl.BlockSpec(memory_space=pl.ANY)] * len(kv_pieces),
            out_specs=pl.BlockSpec((rows_mine, queries.shape[1]), lambda i, *_: (0, 0)),
            scratch_shapes=[
                pltpu.SMEM((n_local, listed), jnp.int32),
                pltpu.VMEM((n_local, listed, BLK, kv_local.shape[1] + HD), jnp.bfloat16),
                pltpu.VMEM((n_local, BLK, kv_local.shape[1]), jnp.bfloat16),
                pltpu.SemaphoreType.DMA((n_local, listed)),
                pltpu.SemaphoreType.DMA((n_local,)),
            ],
        ),
        compiler_params=pltpu.CompilerParams(vmem_limit_bytes=48 * 1024 * 1024),
    )(block_list, block_count, qb0, queries, *kv_pieces)


def solution(mesh):
    placed = (P("pb", None), P(("ka", "pb"), None), P(("ka", "pb"), None), P("pb", None), P("pb"))
    body = functools.partial(shards, n_pb=mesh.shape["pb"], n_ka=mesh.shape["ka"])
    return jax.shard_map(
        body, mesh=mesh, in_specs=placed, out_specs=P(("pb", "ka"), None), check_vma=False
    )
```

```python
import functools
import math

import jax
import jax.numpy as jnp
from jax import lax
from jax.experimental import pallas as pl
from jax.experimental.pallas import tpu as pltpu
from jax.sharding import PartitionSpec as P

HD = 128
QH = 4
BLK = 128

masked_score = -1e30


def gather_axis(local, axis, n):
    idx = lax.axis_index(axis)
    bits = n.bit_length() - 1
    held = local.reshape((1,) * bits + local.shape)
    for t in range(bits):
        b = n >> (t + 1)
        other = lax.ppermute(held, axis, [(i, i ^ b) for i in range(n)])
        upper = (idx // b) % 2 == 1
        held = jnp.where(
            upper,
            jnp.concatenate([other, held], axis=t),
            jnp.concatenate([held, other], axis=t),
        )
    return held.reshape((n * local.shape[0],) + local.shape[1:])


def pieces_axis(local, axis, n):
    idx_pieces = {0: local}
    b = n // 2
    while b >= 1:
        for x in sorted(idx_pieces):
            idx_pieces[x | b] = lax.ppermute(idx_pieces[x], axis, [(i, i ^ b) for i in range(n)])
        b //= 2
    return [idx_pieces[x] for x in range(n)]


def attend_kernel(bl_ref, cnt_ref, qb_ref, q_ref, *rest, n_local, n_pieces, n_ka, group, scale):
    kv_pieces = rest[:n_pieces]
    out_ref, off_ref, kvbuf, dbuf, sems, dsems = rest[n_pieces:]
    qb0 = qb_ref[0]
    me = qb_ref[1]
    row0 = me * n_local
    width = kvbuf.shape[-1]
    per_piece = kv_pieces[0].shape[0] // BLK
    n_half = n_pieces // n_ka

    class block_copy:
        def __init__(self, blk, dst, sem):
            self.blk, self.dst, self.sem = blk, dst, sem

        def start(self):
            per_shard = per_piece * n_half
            within = self.blk % per_shard
            which = (within % n_half) * n_ka + jnp.bitwise_xor(self.blk // per_shard, me)
            start = pl.multiple_of((within // n_half) * BLK, BLK)
            for x in range(n_pieces):
                @pl.when(which == x)
                def _(x=x, start=start):
                    pltpu.make_async_copy(kv_pieces[x].at[pl.ds(start, BLK), :], self.dst, self.sem).start()

        def wait(self):
            pltpu.make_async_copy(kv_pieces[0].at[pl.ds(0, BLK), :], self.dst, self.sem).wait()

    def copy(j, s):
        return block_copy(off_ref[j, s], kvbuf.at[j, s, :, pl.ds(0, 2 * HD)], sems.at[j, s])

    kvbuf[:, :, :, 2 * HD:] = jnp.ones(kvbuf.shape[:3] + (HD,), kvbuf.dtype)

    n_off = []
    for j in range(n_local):
        qb = qb0 + j
        block_copy(qb, dbuf.at[j], dsems.at[j]).start()

        def compact(s, n, j=j, qb=qb):
            b = bl_ref[row0 + j, s]
            off_ref[j, n] = b
            return n + (b != qb).astype(jnp.int32)

        n_j = lax.fori_loop(0, cnt_ref[row0 + j], compact, 0)
        n_off.append(n_j)
        n_pad = (n_j + group - 1) // group * group

        def pad(s, c, j=j, qb=qb):
            off_ref[j, s] = qb
            return c

        lax.fori_loop(n_j, n_pad, pad, 0)

        def issue(s, c, j=j):
            copy(j, s).start()
            return c

        lax.fori_loop(0, n_pad, issue, 0)

    rows = QH * BLK
    rowpos = lax.broadcasted_iota(jnp.int32, (rows, BLK), 0) % BLK
    col = lax.broadcasted_iota(jnp.int32, (rows, BLK), 1)
    causal = col <= rowpos
    dims = (((1,), (1,)), ((), ()))

    slot_of = lax.broadcasted_iota(jnp.int32, (rows, group * BLK), 1) // BLK

    def update(qs, kvb, carry, live=None):
        m, l, acc = carry
        k = kvb[:, :HD]
        v = kvb[:, HD:]
        sc = lax.dot_general(qs, k, dims, preferred_element_type=jnp.float32)
        if live is not None:
            sc = jnp.where(slot_of < live, sc, masked_score)
        m_new = jnp.maximum(m, jnp.max(sc, axis=1, keepdims=True) * scale)
        alpha = jnp.exp2(m - m_new)
        w = jnp.exp2(sc * scale - m_new)
        both = jnp.dot(w.astype(jnp.bfloat16), v, preferred_element_type=jnp.float32)
        l = alpha * l + both[:, HD:HD + 1]
        acc = alpha * acc + both[:, :HD]
        return m_new, l, acc

    for j in range(n_local):
        qb = qb0 + j
        qrows = q_ref[j * BLK:(j + 1) * BLK, :]
        qs = jnp.concatenate([qrows[:, h * HD:(h + 1) * HD] for h in range(QH)], axis=0)

        block_copy(qb, dbuf.at[j], dsems.at[j]).wait()
        kvd = dbuf[j]
        sc = lax.dot_general(qs, kvd[:, :HD], dims, preferred_element_type=jnp.float32) * scale
        m = jnp.max(jnp.where(causal, sc, masked_score), axis=1, keepdims=True)
        w = jnp.where(causal, jnp.exp2(sc - m), 0.0)
        l = jnp.sum(w, axis=1, keepdims=True)
        acc = jnp.dot(w.astype(jnp.bfloat16), kvd[:, HD:2 * HD], preferred_element_type=jnp.float32)

        def grouped(g, carry, j=j, qs=qs):
            first = g * group
            for i in range(group):
                copy(j, first + i).wait()
            kvb = kvbuf[j, pl.ds(first, group)].reshape(group * BLK, width)
            return update(qs, kvb, carry)

        def last(g, carry, j=j, qs=qs):
            first = g * group
            for i in range(group):
                copy(j, first + i).wait()
            kvb = kvbuf[j, pl.ds(first, group)].reshape(group * BLK, width)
            return update(qs, kvb, carry, live=n_off[j] - first)

        n_groups = n_off[j] // group
        carry = lax.fori_loop(0, n_groups, grouped, (m, l, acc))
        m, l, acc = lax.fori_loop(n_groups, (n_off[j] + group - 1) // group, last, carry)
        res = (acc / l).astype(out_ref.dtype)
        for h in range(QH):
            out_ref[j * BLK:(j + 1) * BLK, h * HD:(h + 1) * HD] = res[h * BLK:(h + 1) * BLK, :]


def shards(queries, key_cache, value_cache, block_list, block_count, *, n_pb, n_ka):
    n_half = key_cache.shape[0] // BLK
    width2 = key_cache.shape[1] + value_cache.shape[1]
    kv_pieces = []
    shard = None
    for h in range(n_half):
        part = jnp.concatenate([key_cache[h * BLK:(h + 1) * BLK], value_cache[h * BLK:(h + 1) * BLK]], axis=1)
        if h % 2 == 0:
            shard = gather_axis(part, "pb", n_pb)
            continue
        b = n_ka // 2
        across = lax.ppermute(part, "ka", [(i, i ^ b) for i in range(n_ka)])
        pair, shard = lax.optimization_barrier((jnp.stack([part, across]), shard))
        kv_pieces += pieces_axis(shard, "ka", n_ka)
        shard = None
        both = gather_axis(pair, "pb", n_pb).reshape(n_pb, 2, BLK, part.shape[1])
        held = {0: both[:, 0].reshape(-1, part.shape[1]), b: both[:, 1].reshape(-1, part.shape[1])}
        step = b // 2
        while step >= 1:
            for x in sorted(held):
                held[x | step] = lax.ppermute(held[x], "ka", [(i, i ^ step) for i in range(n_ka)])
            step //= 2
        kv_pieces += [held[x] for x in range(n_ka)]
    if shard is not None:
        kv_pieces += pieces_axis(shard, "ka", n_ka)

    p = lax.axis_index("pb")
    k = lax.axis_index("ka")
    rows_mine = queries.shape[0] // n_ka
    n_local = rows_mine // BLK
    listed = block_list.shape[1]
    qb0 = jnp.stack([(p * n_ka + k) * n_local, k]).astype(jnp.int32)

    kernel = functools.partial(
        attend_kernel, n_local=n_local, n_pieces=len(kv_pieces), n_ka=n_ka, group=16, scale=math.log2(math.e) / math.sqrt(HD)
    )
    return pl.pallas_call(
        kernel,
        out_shape=jax.ShapeDtypeStruct((rows_mine, queries.shape[1]), jnp.bfloat16),
        grid_spec=pltpu.PrefetchScalarGridSpec(
            num_scalar_prefetch=3,
            grid=(1,),
            in_specs=[
                pl.BlockSpec((rows_mine, queries.shape[1]), lambda i, bl, cnt, qb: (qb[1], 0)),
            ]
            + [pl.BlockSpec(memory_space=pl.ANY)] * len(kv_pieces),
            out_specs=pl.BlockSpec((rows_mine, queries.shape[1]), lambda i, *_: (0, 0)),
            scratch_shapes=[
                pltpu.SMEM((n_local, listed), jnp.int32),
                pltpu.VMEM((n_local, listed, BLK, width2 + HD), jnp.bfloat16),
                pltpu.VMEM((n_local, BLK, width2), jnp.bfloat16),
                pltpu.SemaphoreType.DMA((n_local, listed)),
                pltpu.SemaphoreType.DMA((n_local,)),
            ],
        ),
        compiler_params=pltpu.CompilerParams(vmem_limit_bytes=48 * 1024 * 1024),
    )(block_list, block_count, qb0, queries, *kv_pieces)


def solution(mesh):
    placed = (P("pb", None), P(("ka", "pb"), None), P(("ka", "pb"), None), P("pb", None), P("pb"))
    body = functools.partial(shards, n_pb=mesh.shape["pb"], n_ka=mesh.shape["ka"])
    return jax.shard_map(
        body, mesh=mesh, in_specs=placed, out_specs=P(("pb", "ka"), None), check_vma=False
    )
```

```python
import functools
import math

import jax
import jax.numpy as jnp
from jax import lax
from jax.experimental import pallas as pl
from jax.experimental.pallas import tpu as pltpu
from jax.sharding import PartitionSpec as P

HD = 128
QH = 4
BLK = 128

masked_score = -1e30


def gather_axis(local, axis, n):
    idx = lax.axis_index(axis)
    bits = n.bit_length() - 1
    held = local.reshape((1,) * bits + local.shape)
    for t in range(bits):
        b = n >> (t + 1)
        other = lax.ppermute(held, axis, [(i, i ^ b) for i in range(n)])
        upper = (idx // b) % 2 == 1
        held = jnp.where(
            upper,
            jnp.concatenate([other, held], axis=t),
            jnp.concatenate([held, other], axis=t),
        )
    return held.reshape((n * local.shape[0],) + local.shape[1:])


def pieces_axis(local, axis, n):
    idx_pieces = {0: local}
    b = n // 2
    while b >= 1:
        for x in sorted(idx_pieces):
            idx_pieces[x | b] = lax.ppermute(idx_pieces[x], axis, [(i, i ^ b) for i in range(n)])
        b //= 2
    return [idx_pieces[x] for x in range(n)]


def attend_kernel(bl_ref, cnt_ref, qb_ref, q_ref, *rest, n_local, n_pieces, n_ka, group, scale):
    kv_pieces = rest[:n_pieces]
    out_ref, off_ref, kvbuf, dbuf, sems, dsems = rest[n_pieces:]
    qb0 = qb_ref[0]
    me = qb_ref[1]
    row0 = me * n_local
    width = kvbuf.shape[-1]
    per_piece = kv_pieces[0].shape[0] // BLK
    n_half = n_pieces // n_ka

    class block_copy:
        def __init__(self, blk, dst, sem):
            self.blk, self.dst, self.sem = blk, dst, sem

        def start(self):
            per_shard = per_piece * n_half
            within = self.blk % per_shard
            which = (within % n_half) * n_ka + jnp.bitwise_xor(self.blk // per_shard, me)
            start = pl.multiple_of((within // n_half) * BLK, BLK)
            for x in range(n_pieces):
                @pl.when(which == x)
                def _(x=x, start=start):
                    pltpu.make_async_copy(kv_pieces[x].at[pl.ds(start, BLK), :], self.dst, self.sem).start()

        def wait(self):
            pltpu.make_async_copy(kv_pieces[0].at[pl.ds(0, BLK), :], self.dst, self.sem).wait()

    def copy(j, s):
        return block_copy(off_ref[j, s], kvbuf.at[j, s, :, pl.ds(0, 2 * HD)], sems.at[j, s])

    kvbuf[:, :, :, 2 * HD:] = jnp.ones(kvbuf.shape[:3] + (HD,), kvbuf.dtype)

    n_off = []
    for j in range(n_local):
        qb = qb0 + j
        block_copy(qb, dbuf.at[j], dsems.at[j]).start()

        def compact(s, n, j=j, qb=qb):
            b = bl_ref[row0 + j, s]
            off_ref[j, n] = b
            return n + (b != qb).astype(jnp.int32)

        n_j = lax.fori_loop(0, cnt_ref[row0 + j], compact, 0)
        n_off.append(n_j)
        n_pad = (n_j + group - 1) // group * group

        def pad(s, c, j=j, qb=qb):
            off_ref[j, s] = qb
            return c

        lax.fori_loop(n_j, n_pad, pad, 0)

        def issue(s, c, j=j):
            copy(j, s).start()
            return c

        lax.fori_loop(0, n_pad, issue, 0)

    rows = QH * BLK
    rowpos = lax.broadcasted_iota(jnp.int32, (rows, BLK), 0) % BLK
    col = lax.broadcasted_iota(jnp.int32, (rows, BLK), 1)
    causal = col <= rowpos
    dims = (((1,), (1,)), ((), ()))

    slot_of = lax.broadcasted_iota(jnp.int32, (rows, group * BLK), 1) // BLK

    def update(qs, kvb, carry, live=None):
        m, l, acc = carry
        k = kvb[:, :HD]
        v = kvb[:, HD:]
        sc = lax.dot_general(qs, k, dims, preferred_element_type=jnp.float32)
        if live is not None:
            sc = jnp.where(slot_of < live, sc, masked_score)
        m_new = jnp.maximum(m, jnp.max(sc, axis=1, keepdims=True) * scale)
        alpha = jnp.exp2(m - m_new)
        w = jnp.exp2(sc * scale - m_new)
        both = jnp.dot(w.astype(jnp.bfloat16), v, preferred_element_type=jnp.float32)
        l = alpha * l + both[:, HD:HD + 1]
        acc = alpha * acc + both[:, :HD]
        return m_new, l, acc

    for j in range(n_local):
        qb = qb0 + j
        qrows = q_ref[j * BLK:(j + 1) * BLK, :]
        qs = jnp.concatenate([qrows[:, h * HD:(h + 1) * HD] for h in range(QH)], axis=0)

        block_copy(qb, dbuf.at[j], dsems.at[j]).wait()
        kvd = dbuf[j]
        sc = lax.dot_general(qs, kvd[:, :HD], dims, preferred_element_type=jnp.float32) * scale
        m = jnp.max(jnp.where(causal, sc, masked_score), axis=1, keepdims=True)
        w = jnp.where(causal, jnp.exp2(sc - m), 0.0)
        l = jnp.sum(w, axis=1, keepdims=True)
        acc = jnp.dot(w.astype(jnp.bfloat16), kvd[:, HD:2 * HD], preferred_element_type=jnp.float32)

        def grouped(g, carry, j=j, qs=qs):
            first = g * group
            for i in range(group):
                copy(j, first + i).wait()
            kvb = kvbuf[j, pl.ds(first, group)].reshape(group * BLK, width)
            return update(qs, kvb, carry)

        def last(g, carry, j=j, qs=qs):
            first = g * group
            for i in range(group):
                copy(j, first + i).wait()
            kvb = kvbuf[j, pl.ds(first, group)].reshape(group * BLK, width)
            return update(qs, kvb, carry, live=n_off[j] - first)

        n_groups = n_off[j] // group
        carry = lax.fori_loop(0, n_groups, grouped, (m, l, acc))
        m, l, acc = lax.fori_loop(n_groups, (n_off[j] + group - 1) // group, last, carry)
        res = (acc / l).astype(out_ref.dtype)
        for h in range(QH):
            out_ref[j * BLK:(j + 1) * BLK, h * HD:(h + 1) * HD] = res[h * BLK:(h + 1) * BLK, :]


def shards(queries, key_cache, value_cache, block_list, block_count, *, n_pb, n_ka):
    kv_local = jnp.concatenate([key_cache, value_cache], axis=1)
    n_half = kv_local.shape[0] // BLK
    kv_pieces = []
    shard = None
    for h in range(n_half):
        part = kv_local[h * BLK:(h + 1) * BLK]
        if h % 2 == 0:
            shard = gather_axis(part, "pb", n_pb)
            continue
        b = n_ka // 2
        across = lax.ppermute(part, "ka", [(i, i ^ b) for i in range(n_ka)])
        mate = lax.ppermute(shard, "ka", [(i, i ^ 1) for i in range(n_ka)])
        pair, shard, mate = lax.optimization_barrier((jnp.stack([part, across]), shard, mate))
        other = lax.ppermute(shard, "ka", [(i, i ^ b) for i in range(n_ka)])
        kv_pieces += [shard, mate, other, lax.ppermute(other, "ka", [(i, i ^ 1) for i in range(n_ka)])]
        shard = None
        both = gather_axis(pair, "pb", n_pb).reshape(n_pb, 2, BLK, part.shape[1])
        held = {0: both[:, 0].reshape(-1, part.shape[1]), b: both[:, 1].reshape(-1, part.shape[1])}
        step = b // 2
        while step >= 1:
            for x in sorted(held):
                held[x | step] = lax.ppermute(held[x], "ka", [(i, i ^ step) for i in range(n_ka)])
            step //= 2
        kv_pieces += [held[x] for x in range(n_ka)]
    if shard is not None:
        kv_pieces += pieces_axis(shard, "ka", n_ka)

    p = lax.axis_index("pb")
    k = lax.axis_index("ka")
    rows_mine = queries.shape[0] // n_ka
    n_local = rows_mine // BLK
    listed = block_list.shape[1]
    qb0 = jnp.stack([(p * n_ka + k) * n_local, k]).astype(jnp.int32)

    kernel = functools.partial(
        attend_kernel, n_local=n_local, n_pieces=len(kv_pieces), n_ka=n_ka, group=16, scale=math.log2(math.e) / math.sqrt(HD)
    )
    return pl.pallas_call(
        kernel,
        out_shape=jax.ShapeDtypeStruct((rows_mine, queries.shape[1]), jnp.bfloat16),
        grid_spec=pltpu.PrefetchScalarGridSpec(
            num_scalar_prefetch=3,
            grid=(1,),
            in_specs=[
                pl.BlockSpec((rows_mine, queries.shape[1]), lambda i, bl, cnt, qb: (qb[1], 0)),
            ]
            + [pl.BlockSpec(memory_space=pl.ANY)] * len(kv_pieces),
            out_specs=pl.BlockSpec((rows_mine, queries.shape[1]), lambda i, *_: (0, 0)),
            scratch_shapes=[
                pltpu.SMEM((n_local, listed), jnp.int32),
                pltpu.VMEM((n_local, listed, BLK, kv_local.shape[1] + HD), jnp.bfloat16),
                pltpu.VMEM((n_local, BLK, kv_local.shape[1]), jnp.bfloat16),
                pltpu.SemaphoreType.DMA((n_local, listed)),
                pltpu.SemaphoreType.DMA((n_local,)),
            ],
        ),
        compiler_params=pltpu.CompilerParams(vmem_limit_bytes=48 * 1024 * 1024),
    )(block_list, block_count, qb0, queries, *kv_pieces)


def solution(mesh):
    placed = (P("pb", None), P(("ka", "pb"), None), P(("ka", "pb"), None), P("pb", None), P("pb"))
    body = functools.partial(shards, n_pb=mesh.shape["pb"], n_ka=mesh.shape["ka"])
    return jax.shard_map(
        body, mesh=mesh, in_specs=placed, out_specs=P(("pb", "ka"), None), check_vma=False
    )
```
